512 devices in a mesh: tm: 16 (over z, core), space: 32 (over x, y).
Axes of the slice: x: 4, y: 8, z: 8, core: 2. Of those that a mesh axis runs over, the one named last changes fastest.
Arguments:
- hindcast_archive: bfloat16 [16, 4, 16, 4, 32768], P('tm', None, None, None, 'space'), may hold values from -6 to 6
- op_blocks: bfloat16 [16, 3072, 128, 128], P('tm', 'space'), may hold values from -0.5 to 0.5
- block_index: int32 [16, 3072], P('tm', 'space'), may hold values from 0 to 11
- obs_values: bfloat16 [16, 4, 393216], P('tm', None, 'space'), may hold values from -6 to 6
- obs_weights: bfloat16 [16, 4, 393216], P('tm', None, 'space'), may hold values from 0.049804688 to 0.5
- obs_counts: int32 [16, 32], P('tm', 'space'), may hold values from 3072 to 12288, as said below
Outputs:
- gradient: float32 [16, 16, 4, 32768], P('tm', None, None, 'space')
The draws below stay inside these ranges and needn't reach their ends.
Inputs may be any that keep to these rules, and one draw needn't show every extreme that they name: `block_index`: A value below 2 names one of the last 2 blocks of the tile before, a value from 2 to 9 one of the tile's own blocks, a larger one the first blocks of the tile after. `obs_counts`: in every valid time some tile has all 12288 slots live; the live observations of a tile are its first slots.
All inputs are finite; a program needn't handle non-finite values.
Results may differ from the reference program's by a relative error of at most 0.0014.
Values may be sent and summed in bfloat16 or wider, within the bound.
No kernel may reach another device: no remote copies, remote signals or barrier semaphores. Data moves between devices by JAX's collectives and lax.ppermute only.
A program may use at most 128 MiB of HBM per device.

```python
import math
import jax
import jax.numpy as jnp
from jax import lax

L = 4
ENSEMBLE_SIZE = 16
VERTICAL_LAYERS = 4
GROUP_SITE_SPAN = 128
CB_DEV = 8
OB_DEV = 96
EDGE = 2
S = 16
LEAD_STRIDE = 4
TILES = 32
NC = 32768
OBS_DEV = 12288
OBLK = 3072
OBS = 393216
N_SPACE = 32


def draw_obs_counts(key, part):
    first_key, second_key = jax.random.split(jax.random.fold_in(key, 17))
    base = jax.random.randint(first_key, (S, TILES), OBS_DEV // 4, OBS_DEV + 1)
    full_tile = jax.random.randint(second_key, (S,), 0, TILES)
    tile_ids = jnp.arange(TILES, dtype=jnp.int32)[None, :]
    return jnp.where(tile_ids == full_tile[:, None], OBS_DEV, base).astype(jnp.int32)


def touch_ends(array, key, least, largest):
    extent = array.shape
    place = [jax.random.randint(jax.random.fold_in(key, axis), (), 0, extent[axis]) for axis in range(len(extent))]
    array = array.at[tuple(place)].set(least)
    longest = extent.index(max(extent))
    place[longest] = (place[longest] + 1) % extent[longest]
    return array.at[tuple(place)].set(largest)


def block_scale(own_key, shape, pieces, low, high):
    factor_of = 1.0
    for position, blocks in pieces:
        steps = jax.random.uniform(jax.random.fold_in(jax.random.fold_in(own_key, 6), position), (blocks,), jnp.float32, low / len(pieces), high / len(pieces))
        factor_of = factor_of * jnp.repeat(jnp.exp(steps), shape[position] // blocks).reshape((-1,) + (1,) * (len(shape) - 1 - position))
    return factor_of


def normal_values(own_key, extent, spread, most, shards=(), held_as=jnp.bfloat16):
    loudness = block_scale(own_key, extent, shards, -0.22, 0.18) if shards else 1.0
    values = jax.random.normal(own_key, extent, jnp.float32) * spread * loudness
    return jnp.minimum(jnp.maximum(values, -most), most).astype(held_as)


def setup_inputs(seed: int = 0) -> dict:
    key_list = jax.random.split(jax.random.key(seed), 7)
    hindcast_archive = normal_values(key_list[0], (S, L, ENSEMBLE_SIZE, VERTICAL_LAYERS, NC), 1.0, 6.0, ((0, 16), (4, 32)))
    op_blocks = normal_values(key_list[1], (S, OBLK, GROUP_SITE_SPAN, GROUP_SITE_SPAN), GROUP_SITE_SPAN ** -0.5, 0.5, ((0, 16), (1, 32)))
    block_index = touch_ends(jax.random.randint(key_list[2], (S, OBLK), 0, CB_DEV + 2 * EDGE), jax.random.fold_in(key_list[2], 1), 0, (CB_DEV + 2 * EDGE) - 1).astype(jnp.int32)
    obs_values = normal_values(key_list[3], (S, VERTICAL_LAYERS, OBS), 1.0, 6.0, ((0, 16), (2, 32)))
    obs_weights = jnp.clip(jnp.exp(math.log(0.5) - 2.306499 * jax.random.uniform(key_list[4], (S, VERTICAL_LAYERS, OBS), jnp.float32) ** block_scale(key_list[4], (S, VERTICAL_LAYERS, OBS), ((0, 16), (2, 32)), -0.2, 0.2)), 0.049804688, 0.5).astype(jnp.bfloat16)
    obs_counts = draw_obs_counts(jax.random.fold_in(key_list[6], 71), 0)
    return dict(hindcast_archive=hindcast_archive, op_blocks=op_blocks, block_index=block_index, obs_values=obs_values, obs_weights=obs_weights, obs_counts=obs_counts)


def reference(hindcast_archive, op_blocks, block_index, obs_values, obs_weights, obs_counts):
    number_of_groups = CB_DEV * N_SPACE
    owners = jnp.arange(OBLK, dtype=jnp.int32) // OB_DEV
    global_blocks = ((owners * CB_DEV)[None, :] + block_index - EDGE) % number_of_groups
    global_blocks = global_blocks.astype(jnp.int32)
    obs_index = jnp.arange(OBS, dtype=jnp.int32)
    obs_tile = obs_index // OBS_DEV
    obs_slot = obs_index % OBS_DEV
    results = []
    for launch_day in range(S):
        running = jnp.zeros((ENSEMBLE_SIZE * VERTICAL_LAYERS, number_of_groups, GROUP_SITE_SPAN), jnp.float32)
        for horizon_step in range(L):
            valid_time = (launch_day + horizon_step * LEAD_STRIDE) % S
            predicted_model_vector = hindcast_archive[launch_day, horizon_step].astype(jnp.float32).reshape(ENSEMBLE_SIZE * VERTICAL_LAYERS, number_of_groups, GROUP_SITE_SPAN)
            operator = op_blocks[valid_time].astype(jnp.float32)
            picked_matrix_lines = global_blocks[valid_time]
            collected_entries = predicted_model_vector[:, picked_matrix_lines, :]
            images = jnp.einsum("bij,cbj->cbi", operator, collected_entries).reshape(ENSEMBLE_SIZE, VERTICAL_LAYERS, OBS)
            live_mask = (obs_slot < obs_counts[valid_time][obs_tile]).astype(jnp.float32)
            misfit = ((images - obs_values[valid_time].astype(jnp.float32))
                      * obs_weights[valid_time].astype(jnp.float32) * live_mask).astype(jnp.bfloat16)
            misfit = lax.optimization_barrier(misfit)
            adjoint = jnp.einsum("bij,cbi->cbj", operator,
                                 misfit.astype(jnp.float32).reshape(ENSEMBLE_SIZE * VERTICAL_LAYERS, OBLK, GROUP_SITE_SPAN))
            summed = jax.ops.segment_sum(jnp.swapaxes(adjoint, 0, 1), picked_matrix_lines, num_segments=number_of_groups)
            running = running + jnp.swapaxes(summed, 0, 1)
        results.append(running.reshape(ENSEMBLE_SIZE, VERTICAL_LAYERS, number_of_groups * GROUP_SITE_SPAN))
    return jnp.stack(results)
```

```python
import functools

import jax
import jax.numpy as jnp
from jax import lax
from jax.experimental import pallas as pl
from jax.experimental.pallas import tpu as pltpu
from jax.sharding import PartitionSpec as P

GROUP_SITE_SPAN = 128
EDGE = 2
BLOCKS_PER_STEP = 8


def with_halo(block, sides, width):
    for axis, dim in sides:
        count = lax.axis_size(axis)
        forward = [(i, i + 1) for i in range(count - 1)]
        forward.append((count - 1, 0))
        backward = [(target, source) for source, target in forward]
        low = lax.ppermute(
            lax.slice_in_dim(block, block.shape[dim] - width, None, axis=dim), axis, forward
        )
        high = lax.ppermute(lax.slice_in_dim(block, 0, width, axis=dim), axis, backward)
        block = jnp.concatenate([low, block, high], axis=dim)
    return block


def passed_along(value, axis, steps):
    count = lax.axis_size(axis)
    pairs = [(source, (source + steps) % count) for source in range(count)]
    return lax.ppermute(value, axis, pairs)


def extend(grouped):
    return with_halo(grouped, (("space", 4),), EDGE * GROUP_SITE_SPAN)


def observe_kernel(idx_ref, cnt_ref, ext_ref, op_ref, val_ref, wt_ref, out_ref):
    step = pl.program_id(0)
    width = GROUP_SITE_SPAN
    fields = val_ref.shape[0]
    rows = ext_ref.shape[0]

    @pl.when(step == 0)
    def _():
        out_ref[...] = jnp.zeros_like(out_ref)

    count = cnt_ref[0]
    lane = lax.broadcasted_iota(jnp.int32, (1, 1, width), 2)
    for k in range(BLOCKS_PER_STEP):
        b = step * BLOCKS_PER_STEP + k
        start = pl.multiple_of(idx_ref[b] * width, width)
        x = ext_ref[:, pl.ds(start, width)]
        op = op_ref[k]
        images = lax.dot_general(
            x, op, (((1,), (1,)), ((), ())), preferred_element_type=jnp.float32
        ).reshape(fields, rows // fields, width)
        observed = val_ref[:, k * width:(k + 1) * width].astype(jnp.float32)[:, None, :]
        scaling = wt_ref[:, k * width:(k + 1) * width].astype(jnp.float32)[:, None, :]
        live = (b * width + lane) < count
        misfit = jnp.where(live, (images - observed) * scaling, 0.0).astype(jnp.bfloat16)
        adjoint = jnp.dot(
            misfit.reshape(rows, width), op, preferred_element_type=jnp.float32
        )
        out_ref[:, pl.ds(start, width)] += adjoint


def observe(ext_rows, operator, indices, values, weights, counts):
    rows, cells = ext_rows.shape
    obs_blocks = operator.shape[0]
    width = GROUP_SITE_SPAN
    fields = values.shape[0]
    steps = obs_blocks // BLOCKS_PER_STEP
    span = BLOCKS_PER_STEP * width
    grid_spec = pltpu.PrefetchScalarGridSpec(
        num_scalar_prefetch=2,
        grid=(steps,),
        in_specs=[
            pl.BlockSpec((rows, cells), lambda g, i, c: (0, 0)),
            pl.BlockSpec((BLOCKS_PER_STEP, width, width), lambda g, i, c: (g, 0, 0)),
            pl.BlockSpec((fields, span), lambda g, i, c: (0, g)),
            pl.BlockSpec((fields, span), lambda g, i, c: (0, g)),
        ],
        out_specs=pl.BlockSpec((rows, cells), lambda g, i, c: (0, 0)),
    )
    flops = 4 * obs_blocks * rows * width * width
    bytes_accessed = operator.size * 2 + ext_rows.size * 2 + rows * cells * 4 + values.size * 4
    return pl.pallas_call(
        observe_kernel,
        grid_spec=grid_spec,
        out_shape=jax.ShapeDtypeStruct((rows, cells), jnp.float32),
        compiler_params=pltpu.CompilerParams(dimension_semantics=("arbitrary",)),
        cost_estimate=pl.CostEstimate(
            flops=flops, bytes_accessed=bytes_accessed, transcendentals=0
        ),
    )(indices, counts, ext_rows, operator, values, weights)


def settle(adjoint_ext):
    rim_width = EDGE * GROUP_SITE_SPAN
    lower_rim = adjoint_ext[..., :rim_width]
    upper_rim = adjoint_ext[..., -rim_width:]
    interior = adjoint_ext[..., rim_width:-rim_width]
    from_above = passed_along(lower_rim, "space", -1)
    from_below = passed_along(upper_rim, "space", 1)
    interior = interior.at[..., -rim_width:].add(from_above)
    return interior.at[..., :rim_width].add(from_below)


def body(hindcast_archive, op_blocks, block_index, obs_values, obs_weights, obs_counts):
    tm_size = lax.axis_size("tm")
    lead_count = hindcast_archive.shape[1]
    regrouped = [hindcast_archive[:, 0]]
    for horizon_step in range(1, lead_count):
        regrouped.append(
            passed_along(
                hindcast_archive[:, horizon_step], "tm", horizon_step * tm_size // lead_count
            )
        )
    extended = extend(jnp.stack(regrouped, axis=1))[0]
    leads, members, fields, cells = extended.shape
    ext_rows = jnp.transpose(extended, (2, 0, 1, 3)).reshape(fields * leads * members, cells)
    adjoint_rows = observe(
        ext_rows, op_blocks[0], block_index[0], obs_values[0], obs_weights[0], obs_counts[0]
    )
    adjoint_ext = jnp.transpose(
        adjoint_rows.reshape(fields, leads, members, cells), (1, 2, 0, 3)
    )[None]
    interior = settle(adjoint_ext)
    running = interior[:, 0]
    for horizon_step in range(1, lead_count):
        running = running + passed_along(
            interior[:, horizon_step], "tm", -(horizon_step * tm_size // lead_count)
        )
    return running


def solution(mesh):
    in_specs = (
        P("tm", None, None, None, "space"),
        P("tm", "space", None, None),
        P("tm", "space"),
        P("tm", None, "space"),
        P("tm", None, "space"),
        P("tm", "space"),
    )
    out_specs = P("tm", None, None, "space")
    return jax.shard_map(body, mesh=mesh, in_specs=in_specs, out_specs=out_specs, check_vma=False)
```

```python
import jax
import jax.numpy as jnp
from jax import lax
from jax.experimental import pallas as pl
from jax.experimental.pallas import tpu as pltpu
from jax.sharding import Mesh
from jax.sharding import PartitionSpec as P

GROUP_SITE_SPAN = 128
EDGE = 2
BLOCKS_PER_STEP = 8


def ring_pairs(count, steps):
    return [(source, (source + steps) % count) for source in range(count)]


def observe_kernel(members, idx_ref, cnt_ref, ext_ref, op_ref, val_ref, wt_ref, out_ref):
    step = pl.program_id(0)
    width = GROUP_SITE_SPAN
    fields = val_ref.shape[0]
    rows = ext_ref.shape[0]

    @pl.when(step == 0)
    def _():
        out_ref[...] = jnp.zeros_like(out_ref)

    count = cnt_ref[0]
    lane = lax.broadcasted_iota(jnp.int32, (1, 1, 1, width), 3)
    for k in range(BLOCKS_PER_STEP):
        b = step * BLOCKS_PER_STEP + k
        start = pl.multiple_of(idx_ref[b] * width, width)
        x = ext_ref[:, pl.ds(start, width)]
        op = op_ref[k]
        images = lax.dot_general(
            x, op, (((1,), (1,)), ((), ())), preferred_element_type=jnp.float32
        ).reshape(rows // (fields * members), fields, members, width)
        observed = val_ref[:, k * width:(k + 1) * width].astype(jnp.float32)[None, :, None, :]
        scaling = wt_ref[:, k * width:(k + 1) * width].astype(jnp.float32)[None, :, None, :]
        live = (b * width + lane) < count
        misfit = jnp.where(live, (images - observed) * scaling, 0.0)
        misfit = misfit.reshape(rows, width).astype(jnp.bfloat16)
        adjoint = jnp.dot(misfit, op, preferred_element_type=jnp.float32)
        out_ref[:, pl.ds(start, width)] += adjoint


def observe(ext_rows, operator, indices, values, weights, counts, members):
    rows, cells = ext_rows.shape
    obs_blocks = operator.shape[0]
    width = GROUP_SITE_SPAN
    fields = values.shape[0]
    steps = obs_blocks // BLOCKS_PER_STEP
    span = BLOCKS_PER_STEP * width
    grid_spec = pltpu.PrefetchScalarGridSpec(
        num_scalar_prefetch=2,
        grid=(steps,),
        in_specs=[
            pl.BlockSpec((rows, cells), lambda g, i, c: (0, 0)),
            pl.BlockSpec((BLOCKS_PER_STEP, width, width), lambda g, i, c: (g, 0, 0)),
            pl.BlockSpec((fields, span), lambda g, i, c: (0, g)),
            pl.BlockSpec((fields, span), lambda g, i, c: (0, g)),
        ],
        out_specs=pl.BlockSpec((rows, cells), lambda g, i, c: (0, 0)),
    )
    flops = 4 * obs_blocks * rows * width * width
    bytes_accessed = operator.size * 2 + ext_rows.size * 2 + rows * cells * 4 + values.size * 4
    return pl.pallas_call(
        lambda *refs: observe_kernel(members, *refs),
        grid_spec=grid_spec,
        out_shape=jax.ShapeDtypeStruct((rows, cells), jnp.float32),
        compiler_params=pltpu.CompilerParams(dimension_semantics=("arbitrary",)),
        cost_estimate=pl.CostEstimate(
            flops=flops, bytes_accessed=bytes_accessed, transcendentals=0
        ),
    )(indices, counts, ext_rows, operator, values, weights)


def body(hindcast_archive, op_blocks, block_index, obs_values, obs_weights, obs_counts):
    rim = EDGE * GROUP_SITE_SPAN
    space = lax.axis_size("space")
    ring = lax.axis_size("tq")
    here = lax.axis_index("tq")
    own = hindcast_archive[0]
    leads, members, fields, cells = own.shape
    low = lax.ppermute(own[..., cells - rim:], "space", ring_pairs(space, 1))
    high = lax.ppermute(own[..., :rim], "space", ring_pairs(space, -1))
    extended = jnp.concatenate([low, own, high], axis=-1)
    extended = jnp.transpose(extended, (0, 2, 1, 3))
    outgoing = jnp.roll(extended, here, axis=0)
    incoming = lax.all_to_all(outgoing, "tq", 0, 0, tiled=True)
    width = cells + 2 * rim
    adjoint_rows = observe(
        incoming.reshape(leads * fields * members, width),
        op_blocks[0],
        block_index[0],
        obs_values[0],
        obs_weights[0],
        obs_counts[0],
        members,
    )
    summed = lax.psum_scatter(
        adjoint_rows.reshape(ring, fields * members, width), "tq", scatter_dimension=0, tiled=True
    )[0]
    from_above = lax.ppermute(summed[:, :rim], "space", ring_pairs(space, -1))
    from_below = lax.ppermute(summed[:, width - rim:], "space", ring_pairs(space, 1))
    interior = summed[:, rim:width - rim]
    interior = interior.at[:, cells - rim:].add(from_above)
    interior = interior.at[:, :rim].add(from_below)
    gradient = jnp.transpose(interior.reshape(fields, members, cells), (1, 0, 2))
    return gradient[None]


def solution(mesh):
    tm_size = mesh.shape["tm"]
    lead_count = 4
    devices = mesh.devices.reshape(lead_count, tm_size // lead_count, mesh.shape["space"])
    ring_mesh = Mesh(devices, ("tq", "tr", "space"))
    tm = ("tq", "tr")
    in_specs = (
        P(tm, None, None, None, "space"),
        P(tm, "space", None, None),
        P(tm, "space"),
        P(tm, None, "space"),
        P(tm, None, "space"),
        P(tm, "space"),
    )
    out_specs = P(tm, None, None, "space")
    return jax.shard_map(body, mesh=ring_mesh, in_specs=in_specs, out_specs=out_specs, check_vma=False)
```

```python
import functools

import jax
import jax.numpy as jnp
from jax import lax
from jax.experimental import pallas as pl
from jax.experimental.pallas import tpu as pltpu
from jax.sharding import PartitionSpec as P

GROUP_SITE_SPAN = 128
EDGE = 2
BLOCKS_PER_STEP = 16


def with_halo(block, sides, width):
    for axis, dim in sides:
        count = lax.axis_size(axis)
        forward = [(i, i + 1) for i in range(count - 1)]
        forward.append((count - 1, 0))
        backward = [(target, source) for source, target in forward]
        low = lax.ppermute(
            lax.slice_in_dim(block, block.shape[dim] - width, None, axis=dim), axis, forward
        )
        high = lax.ppermute(lax.slice_in_dim(block, 0, width, axis=dim), axis, backward)
        block = jnp.concatenate([low, block, high], axis=dim)
    return block


def passed_along(value, axis, steps):
    count = lax.axis_size(axis)
    pairs = [(source, (source + steps) % count) for source in range(count)]
    return lax.ppermute(value, axis, pairs)


def extend(grouped):
    return with_halo(grouped, (("space", 4),), EDGE * GROUP_SITE_SPAN)


def observe_kernel(idx_ref, cnt_ref, ext_ref, op_ref, val_ref, wt_ref, out_ref):
    step = pl.program_id(0)
    width = GROUP_SITE_SPAN
    fields = val_ref.shape[0]
    rows = ext_ref.shape[0]

    @pl.when(step == 0)
    def _():
        out_ref[...] = jnp.zeros_like(out_ref)

    count = cnt_ref[0]
    pair = 2 * width
    lane = lax.broadcasted_iota(jnp.int32, (1, 1, pair), 2)
    zero = jnp.zeros((width, width), op_ref.dtype)
    for k in range(0, BLOCKS_PER_STEP, 2):
        b = step * BLOCKS_PER_STEP + k
        first = pl.multiple_of(idx_ref[b] * width, width)
        second = pl.multiple_of(idx_ref[b + 1] * width, width)
        x = jnp.concatenate(
            [ext_ref[:, pl.ds(first, width)], ext_ref[:, pl.ds(second, width)]], axis=1
        )
        op = jnp.concatenate(
            [
                jnp.concatenate([op_ref[k], zero], axis=1),
                jnp.concatenate([zero, op_ref[k + 1]], axis=1),
            ],
            axis=0,
        )
        images = lax.dot_general(
            x, op, (((1,), (1,)), ((), ())), preferred_element_type=jnp.float32
        ).reshape(fields, rows // fields, pair)
        observed = val_ref[:, k * width:k * width + pair].astype(jnp.float32)[:, None, :]
        scaling = wt_ref[:, k * width:k * width + pair].astype(jnp.float32)[:, None, :]
        live = (b * width + lane) < count
        misfit = jnp.where(live, (images - observed) * scaling, 0.0).astype(jnp.bfloat16)
        adjoint = jnp.dot(
            misfit.reshape(rows, pair), op, preferred_element_type=jnp.float32
        )
        out_ref[:, pl.ds(first, width)] += adjoint[:, :width]
        out_ref[:, pl.ds(second, width)] += adjoint[:, width:]


def observe(ext_rows, operator, indices, values, weights, counts):
    rows, cells = ext_rows.shape
    obs_blocks = operator.shape[0]
    width = GROUP_SITE_SPAN
    fields = values.shape[0]
    steps = obs_blocks // BLOCKS_PER_STEP
    span = BLOCKS_PER_STEP * width
    grid_spec = pltpu.PrefetchScalarGridSpec(
        num_scalar_prefetch=2,
        grid=(steps,),
        in_specs=[
            pl.BlockSpec((rows, cells), lambda g, i, c: (0, 0)),
            pl.BlockSpec((BLOCKS_PER_STEP, width, width), lambda g, i, c: (g, 0, 0)),
            pl.BlockSpec((fields, span), lambda g, i, c: (0, g)),
            pl.BlockSpec((fields, span), lambda g, i, c: (0, g)),
        ],
        out_specs=pl.BlockSpec((rows, cells), lambda g, i, c: (0, 0)),
    )
    flops = 4 * obs_blocks * rows * width * width
    bytes_accessed = operator.size * 2 + ext_rows.size * 2 + rows * cells * 4 + values.size * 4
    return pl.pallas_call(
        observe_kernel,
        grid_spec=grid_spec,
        out_shape=jax.ShapeDtypeStruct((rows, cells), jnp.float32),
        compiler_params=pltpu.CompilerParams(dimension_semantics=("arbitrary",)),
        cost_estimate=pl.CostEstimate(
            flops=flops, bytes_accessed=bytes_accessed, transcendentals=0
        ),
    )(indices, counts, ext_rows, operator, values, weights)


def settle(adjoint_ext):
    rim_width = EDGE * GROUP_SITE_SPAN
    lower_rim = adjoint_ext[..., :rim_width]
    upper_rim = adjoint_ext[..., -rim_width:]
    interior = adjoint_ext[..., rim_width:-rim_width]
    from_above = passed_along(lower_rim, "space", -1)
    from_below = passed_along(upper_rim, "space", 1)
    interior = interior.at[..., -rim_width:].add(from_above)
    return interior.at[..., :rim_width].add(from_below)


def body(hindcast_archive, op_blocks, block_index, obs_values, obs_weights, obs_counts):
    tm_size = lax.axis_size("tm")
    lead_count = hindcast_archive.shape[1]
    regrouped = [hindcast_archive[:, 0]]
    for horizon_step in range(1, lead_count):
        regrouped.append(
            passed_along(
                hindcast_archive[:, horizon_step], "tm", horizon_step * tm_size // lead_count
            )
        )
    extended = extend(jnp.stack(regrouped, axis=1))[0]
    leads, members, fields, cells = extended.shape
    ext_rows = jnp.transpose(extended, (2, 0, 1, 3)).reshape(fields * leads * members, cells)
    adjoint_rows = observe(
        ext_rows, op_blocks[0], block_index[0], obs_values[0], obs_weights[0], obs_counts[0]
    )
    adjoint_ext = jnp.transpose(
        adjoint_rows.reshape(fields, leads, members, cells), (1, 2, 0, 3)
    )[None]
    interior = settle(adjoint_ext)
    running = interior[:, 0]
    for horizon_step in range(1, lead_count):
        running = running + passed_along(
            interior[:, horizon_step], "tm", -(horizon_step * tm_size // lead_count)
        )
    return running


def solution(mesh):
    in_specs = (
        P("tm", None, None, None, "space"),
        P("tm", "space", None, None),
        P("tm", "space"),
        P("tm", None, "space"),
        P("tm", None, "space"),
        P("tm", "space"),
    )
    out_specs = P("tm", None, None, "space")
    return jax.shard_map(body, mesh=mesh, in_specs=in_specs, out_specs=out_specs, check_vma=False)
```

```python
import functools

import jax
import jax.numpy as jnp
from jax import lax
from jax.experimental import pallas as pl
from jax.experimental.pallas import tpu as pltpu
from jax.sharding import PartitionSpec as P

GROUP_SITE_SPAN = 128
EDGE = 2
BLOCKS_PER_STEP = 16


def with_halo(block, sides, width):
    for axis, dim in sides:
        count = lax.axis_size(axis)
        forward = [(i, i + 1) for i in range(count - 1)]
        forward.append((count - 1, 0))
        backward = [(target, source) for source, target in forward]
        low = lax.ppermute(
            lax.slice_in_dim(block, block.shape[dim] - width, None, axis=dim), axis, forward
        )
        high = lax.ppermute(lax.slice_in_dim(block, 0, width, axis=dim), axis, backward)
        block = jnp.concatenate([low, block, high], axis=dim)
    return block


def passed_along(value, axis, steps):
    count = lax.axis_size(axis)
    pairs = [(source, (source + steps) % count) for source in range(count)]
    return lax.ppermute(value, axis, pairs)


def extend(grouped):
    return with_halo(grouped, (("space", 4),), EDGE * GROUP_SITE_SPAN)


def observe_kernel(idx_ref, cnt_ref, ext_ref, op_ref, val_ref, wt_ref, out_ref):
    step = pl.program_id(0)
    width = GROUP_SITE_SPAN
    fields = val_ref.shape[0]
    rows = ext_ref.shape[0]

    @pl.when(step == 0)
    def _():
        out_ref[...] = jnp.zeros_like(out_ref)

    count = cnt_ref[0]
    pair = 2 * width
    period = 8
    lane = lax.broadcasted_iota(jnp.int32, (1, 1, pair), 2)
    zero = jnp.zeros((width, width), op_ref.dtype)
    for k in range(0, BLOCKS_PER_STEP, 2):
        b = step * BLOCKS_PER_STEP + k
        first = pl.multiple_of(idx_ref[b] * width, width)
        second = pl.multiple_of(idx_ref[b + 1] * width, width)
        x = jnp.concatenate(
            [ext_ref[:, pl.ds(first, width)], ext_ref[:, pl.ds(second, width)]], axis=1
        )
        op = jnp.concatenate(
            [
                jnp.concatenate([op_ref[k], zero], axis=1),
                jnp.concatenate([zero, op_ref[k + 1]], axis=1),
            ],
            axis=0,
        )
        images = lax.dot_general(
            x, op, (((1,), (1,)), ((), ())), preferred_element_type=jnp.float32
        ).reshape(rows // period, period, pair)
        observed = val_ref[:, k * width:k * width + pair].astype(jnp.float32)
        observed = jnp.concatenate([observed] * (period // fields), axis=0)[None]
        scaling = wt_ref[:, k * width:k * width + pair].astype(jnp.float32)
        scaling = jnp.concatenate([scaling] * (period // fields), axis=0)[None]
        live = (b * width + lane) < count
        misfit = jnp.where(live, (images - observed) * scaling, 0.0).astype(jnp.bfloat16)
        adjoint = jnp.dot(
            misfit.reshape(rows, pair), op, preferred_element_type=jnp.float32
        )
        out_ref[:, pl.ds(first, width)] += adjoint[:, :width]
        out_ref[:, pl.ds(second, width)] += adjoint[:, width:]


def observe(ext_rows, operator, indices, values, weights, counts):
    rows, cells = ext_rows.shape
    obs_blocks = operator.shape[0]
    width = GROUP_SITE_SPAN
    fields = values.shape[0]
    steps = obs_blocks // BLOCKS_PER_STEP
    span = BLOCKS_PER_STEP * width
    grid_spec = pltpu.PrefetchScalarGridSpec(
        num_scalar_prefetch=2,
        grid=(steps,),
        in_specs=[
            pl.BlockSpec((rows, cells), lambda g, i, c: (0, 0)),
            pl.BlockSpec((BLOCKS_PER_STEP, width, width), lambda g, i, c: (g, 0, 0)),
            pl.BlockSpec((fields, span), lambda g, i, c: (0, g)),
            pl.BlockSpec((fields, span), lambda g, i, c: (0, g)),
        ],
        out_specs=pl.BlockSpec((rows, cells), lambda g, i, c: (0, 0)),
    )
    flops = 4 * obs_blocks * rows * width * width
    bytes_accessed = operator.size * 2 + ext_rows.size * 2 + rows * cells * 4 + values.size * 4
    return pl.pallas_call(
        observe_kernel,
        grid_spec=grid_spec,
        out_shape=jax.ShapeDtypeStruct((rows, cells), jnp.float32),
        compiler_params=pltpu.CompilerParams(dimension_semantics=("arbitrary",)),
        cost_estimate=pl.CostEstimate(
            flops=flops, bytes_accessed=bytes_accessed, transcendentals=0
        ),
    )(indices, counts, ext_rows, operator, values, weights)


def settle(adjoint_ext):
    rim_width = EDGE * GROUP_SITE_SPAN
    lower_rim = adjoint_ext[..., :rim_width]
    upper_rim = adjoint_ext[..., -rim_width:]
    interior = adjoint_ext[..., rim_width:-rim_width]
    from_above = passed_along(lower_rim, "space", -1)
    from_below = passed_along(upper_rim, "space", 1)
    interior = interior.at[..., -rim_width:].add(from_above)
    return interior.at[..., :rim_width].add(from_below)


def body(hindcast_archive, op_blocks, block_index, obs_values, obs_weights, obs_counts):
    tm_size = lax.axis_size("tm")
    lead_count = hindcast_archive.shape[1]
    regrouped = [hindcast_archive[:, 0]]
    for horizon_step in range(1, lead_count):
        regrouped.append(
            passed_along(
                hindcast_archive[:, horizon_step], "tm", horizon_step * tm_size // lead_count
            )
        )
    extended = extend(jnp.stack(regrouped, axis=1))[0]
    leads, members, fields, cells = extended.shape
    ext_rows = extended.reshape(leads * members * fields, cells)
    adjoint_rows = observe(
        ext_rows, op_blocks[0], block_index[0], obs_values[0], obs_weights[0], obs_counts[0]
    )
    adjoint_ext = adjoint_rows.reshape(leads, members, fields, cells)[None]
    interior = settle(adjoint_ext)
    running = interior[:, 0]
    for horizon_step in range(1, lead_count):
        running = running + passed_along(
            interior[:, horizon_step], "tm", -(horizon_step * tm_size // lead_count)
        )
    return running


def solution(mesh):
    in_specs = (
        P("tm", None, None, None, "space"),
        P("tm", "space", None, None),
        P("tm", "space"),
        P("tm", None, "space"),
        P("tm", None, "space"),
        P("tm", "space"),
    )
    out_specs = P("tm", None, None, "space")
    return jax.shard_map(body, mesh=mesh, in_specs=in_specs, out_specs=out_specs, check_vma=False)
```

```python
import functools

import jax
import jax.numpy as jnp
from jax import lax
from jax.experimental import pallas as pl
from jax.experimental.pallas import tpu as pltpu
from jax.sharding import Mesh
from jax.sharding import PartitionSpec as P

GROUP_SITE_SPAN = 128
EDGE = 2
BLOCKS_PER_STEP = 16


def with_halo(block, sides, width):
    for axis, dim in sides:
        count = lax.axis_size(axis)
        forward = [(i, i + 1) for i in range(count - 1)]
        forward.append((count - 1, 0))
        backward = [(target, source) for source, target in forward]
        low = lax.ppermute(
            lax.slice_in_dim(block, block.shape[dim] - width, None, axis=dim), axis, forward
        )
        high = lax.ppermute(lax.slice_in_dim(block, 0, width, axis=dim), axis, backward)
        block = jnp.concatenate([low, block, high], axis=dim)
    return block


def passed_along(value, axis, steps):
    count = lax.axis_size(axis)
    pairs = [(source, (source + steps) % count) for source in range(count)]
    return lax.ppermute(value, axis, pairs)


def extend(grouped):
    return with_halo(grouped, (("space", 4),), EDGE * GROUP_SITE_SPAN)


def observe_kernel(idx_ref, cnt_ref, ext_ref, op_ref, val_ref, wt_ref, out_ref):
    step = pl.program_id(0)
    width = GROUP_SITE_SPAN
    fields = val_ref.shape[0]
    rows = ext_ref.shape[0]

    @pl.when(step == 0)
    def _():
        out_ref[...] = jnp.zeros_like(out_ref)

    count = cnt_ref[0]
    pair = 2 * width
    period = 8
    lane = lax.broadcasted_iota(jnp.int32, (1, 1, pair), 2)
    zero = jnp.zeros((width, width), op_ref.dtype)
    for k in range(0, BLOCKS_PER_STEP, 2):
        b = step * BLOCKS_PER_STEP + k
        first = pl.multiple_of(idx_ref[b] * width, width)
        second = pl.multiple_of(idx_ref[b + 1] * width, width)
        x = jnp.concatenate(
            [ext_ref[:, pl.ds(first, width)], ext_ref[:, pl.ds(second, width)]], axis=1
        )
        op = jnp.concatenate(
            [
                jnp.concatenate([op_ref[k], zero], axis=1),
                jnp.concatenate([zero, op_ref[k + 1]], axis=1),
            ],
            axis=0,
        )
        images = lax.dot_general(
            x, op, (((1,), (1,)), ((), ())), preferred_element_type=jnp.float32
        ).reshape(rows // period, period, pair)
        observed = val_ref[:, k * width:k * width + pair].astype(jnp.float32)
        observed = jnp.concatenate([observed] * (period // fields), axis=0)[None]
        scaling = wt_ref[:, k * width:k * width + pair].astype(jnp.float32)
        scaling = jnp.concatenate([scaling] * (period // fields), axis=0)[None]
        live = (b * width + lane) < count
        misfit = jnp.where(live, (images - observed) * scaling, 0.0).astype(jnp.bfloat16)
        adjoint = jnp.dot(
            misfit.reshape(rows, pair), op, preferred_element_type=jnp.float32
        )
        out_ref[:, pl.ds(first, width)] += adjoint[:, :width]
        out_ref[:, pl.ds(second, width)] += adjoint[:, width:]


def observe(ext_rows, operator, indices, values, weights, counts):
    rows, cells = ext_rows.shape
    obs_blocks = operator.shape[0]
    width = GROUP_SITE_SPAN
    fields = values.shape[0]
    steps = obs_blocks // BLOCKS_PER_STEP
    span = BLOCKS_PER_STEP * width
    grid_spec = pltpu.PrefetchScalarGridSpec(
        num_scalar_prefetch=2,
        grid=(steps,),
        in_specs=[
            pl.BlockSpec((rows, cells), lambda g, i, c: (0, 0)),
            pl.BlockSpec((BLOCKS_PER_STEP, width, width), lambda g, i, c: (g, 0, 0)),
            pl.BlockSpec((fields, span), lambda g, i, c: (0, g)),
            pl.BlockSpec((fields, span), lambda g, i, c: (0, g)),
        ],
        out_specs=pl.BlockSpec((rows, cells), lambda g, i, c: (0, 0)),
    )
    flops = 4 * obs_blocks * rows * width * width
    bytes_accessed = operator.size * 2 + ext_rows.size * 2 + rows * cells * 4 + values.size * 4
    return pl.pallas_call(
        observe_kernel,
        grid_spec=grid_spec,
        out_shape=jax.ShapeDtypeStruct((rows, cells), jnp.float32),
        compiler_params=pltpu.CompilerParams(dimension_semantics=("arbitrary",)),
        cost_estimate=pl.CostEstimate(
            flops=flops, bytes_accessed=bytes_accessed, transcendentals=0
        ),
    )(indices, counts, ext_rows, operator, values, weights)


def settle(adjoint_ext):
    rim_width = EDGE * GROUP_SITE_SPAN
    lower_rim = adjoint_ext[..., :rim_width]
    upper_rim = adjoint_ext[..., -rim_width:]
    interior = adjoint_ext[..., rim_width:-rim_width]
    from_above = passed_along(lower_rim, "space", -1)
    from_below = passed_along(upper_rim, "space", 1)
    interior = interior.at[..., -rim_width:].add(from_above)
    return interior.at[..., :rim_width].add(from_below)


def body(hindcast_archive, op_blocks, block_index, obs_values, obs_weights, obs_counts):
    ring = lax.axis_size("tq")
    here = lax.axis_index("tq")
    own = hindcast_archive[0]
    outgoing = jnp.roll(own, here, axis=0)
    incoming = lax.all_to_all(outgoing, "tq", 0, 0, tiled=True)
    extended = extend(incoming[None])[0]
    leads, members, fields, cells = extended.shape
    ext_rows = extended.reshape(leads * members * fields, cells)
    adjoint_rows = observe(
        ext_rows, op_blocks[0], block_index[0], obs_values[0], obs_weights[0], obs_counts[0]
    )
    adjoint_ext = adjoint_rows.reshape(leads, members, fields, cells)[None]
    interior = settle(adjoint_ext)[0]
    running = lax.dynamic_index_in_dim(interior, here, axis=0, keepdims=False)
    for shift in range(1, ring):
        back = lax.dynamic_index_in_dim(interior, (here - shift) % ring, axis=0, keepdims=False)
        running = running + passed_along(back, "tq", -shift)
    return running[None]


def solution(mesh):
    tm_size = mesh.shape["tm"]
    lead_count = 4
    devices = mesh.devices.reshape(lead_count, tm_size // lead_count, mesh.shape["space"])
    ring_mesh = Mesh(devices, ("tq", "tr", "space"))
    tm = ("tq", "tr")
    in_specs = (
        P(tm, None, None, None, "space"),
        P(tm, "space", None, None),
        P(tm, "space"),
        P(tm, None, "space"),
        P(tm, None, "space"),
        P(tm, "space"),
    )
    out_specs = P(tm, None, None, "space")
    return jax.shard_map(body, mesh=ring_mesh, in_specs=in_specs, out_specs=out_specs, check_vma=False)
```

```python
import functools

import jax
import jax.numpy as jnp
from jax import lax
from jax.experimental import pallas as pl
from jax.experimental.pallas import tpu as pltpu
from jax.sharding import Mesh
from jax.sharding import PartitionSpec as P

GROUP_SITE_SPAN = 128
EDGE = 2
BLOCKS_PER_STEP = 32


def with_halo(block, sides, width):
    for axis, dim in sides:
        count = lax.axis_size(axis)
        forward = [(i, i + 1) for i in range(count - 1)]
        forward.append((count - 1, 0))
        backward = [(target, source) for source, target in forward]
        low = lax.ppermute(
            lax.slice_in_dim(block, block.shape[dim] - width, None, axis=dim), axis, forward
        )
        high = lax.ppermute(lax.slice_in_dim(block, 0, width, axis=dim), axis, backward)
        block = jnp.concatenate([low, block, high], axis=dim)
    return block


def passed_along(value, axis, steps):
    count = lax.axis_size(axis)
    pairs = [(source, (source + steps) % count) for source in range(count)]
    return lax.ppermute(value, axis, pairs)


def extend(grouped):
    return with_halo(grouped, (("space", 4),), EDGE * GROUP_SITE_SPAN)


def observe_kernel(idx_ref, cnt_ref, ext_ref, op_ref, val_ref, wt_ref, out_ref):
    step = pl.program_id(0)
    width = GROUP_SITE_SPAN
    fields = val_ref.shape[0]
    rows = ext_ref.shape[0]
    period = 8

    @pl.when(step == 0)
    def _():
        out_ref[...] = jnp.zeros_like(out_ref)

    count = cnt_ref[0]
    lane = lax.broadcasted_iota(jnp.int32, (1, width), 1)
    for k in range(BLOCKS_PER_STEP):
        b = step * BLOCKS_PER_STEP + k
        start = pl.multiple_of(idx_ref[b] * width, width)
        x = ext_ref[:, pl.ds(start, width)]
        op = op_ref[k]
        images = lax.dot_general(
            x, op, (((1,), (1,)), ((), ())), preferred_element_type=jnp.float32
        ).reshape(rows // period, period, width)
        observed = val_ref[:, k * width:(k + 1) * width].astype(jnp.float32)
        observed = jnp.concatenate([observed] * (period // fields), axis=0)[None]
        live = (b * width + lane) < count
        scaling = jnp.where(live, wt_ref[:, k * width:(k + 1) * width].astype(jnp.float32), 0.0)
        scaling = jnp.concatenate([scaling] * (period // fields), axis=0)[None]
        misfit = ((images - observed) * scaling).reshape(rows, width).astype(jnp.bfloat16)
        adjoint = jnp.dot(misfit, op, preferred_element_type=jnp.float32)
        out_ref[:, pl.ds(start, width)] += adjoint


def observe(ext_rows, operator, indices, values, weights, counts):
    rows, cells = ext_rows.shape
    obs_blocks = operator.shape[0]
    width = GROUP_SITE_SPAN
    fields = values.shape[0]
    steps = obs_blocks // BLOCKS_PER_STEP
    span = BLOCKS_PER_STEP * width
    grid_spec = pltpu.PrefetchScalarGridSpec(
        num_scalar_prefetch=2,
        grid=(steps,),
        in_specs=[
            pl.BlockSpec((rows, cells), lambda g, i, c: (0, 0)),
            pl.BlockSpec((BLOCKS_PER_STEP, width, width), lambda g, i, c: (g, 0, 0)),
            pl.BlockSpec((fields, span), lambda g, i, c: (0, g)),
            pl.BlockSpec((fields, span), lambda g, i, c: (0, g)),
        ],
        out_specs=pl.BlockSpec((rows, cells), lambda g, i, c: (0, 0)),
    )
    flops = 4 * obs_blocks * rows * width * width
    bytes_accessed = operator.size * 2 + ext_rows.size * 2 + rows * cells * 4 + values.size * 4
    return pl.pallas_call(
        observe_kernel,
        grid_spec=grid_spec,
        out_shape=jax.ShapeDtypeStruct((rows, cells), jnp.float32),
        compiler_params=pltpu.CompilerParams(dimension_semantics=("arbitrary",)),
        cost_estimate=pl.CostEstimate(
            flops=flops, bytes_accessed=bytes_accessed, transcendentals=0
        ),
    )(indices, counts, ext_rows, operator, values, weights)


def settle(adjoint_ext):
    rim_width = EDGE * GROUP_SITE_SPAN
    lower_rim = adjoint_ext[..., :rim_width]
    upper_rim = adjoint_ext[..., -rim_width:]
    interior = adjoint_ext[..., rim_width:-rim_width]
    from_above = passed_along(lower_rim, "space", -1)
    from_below = passed_along(upper_rim, "space", 1)
    interior = interior.at[..., -rim_width:].add(from_above)
    return interior.at[..., :rim_width].add(from_below)


def body(hindcast_archive, op_blocks, block_index, obs_values, obs_weights, obs_counts):
    ring = lax.axis_size("tq")
    here = lax.axis_index("tq")
    own = hindcast_archive[0]
    outgoing = jnp.roll(own, here, axis=0)
    incoming = lax.all_to_all(outgoing, "tq", 0, 0, tiled=True)
    extended = extend(incoming[None])[0]
    leads, members, fields, cells = extended.shape
    ext_rows = extended.reshape(leads * members * fields, cells)
    adjoint_rows = observe(
        ext_rows, op_blocks[0], block_index[0], obs_values[0], obs_weights[0], obs_counts[0]
    )
    adjoint_ext = adjoint_rows.reshape(leads, members, fields, cells)[None]
    interior = settle(adjoint_ext)[0]
    running = lax.dynamic_index_in_dim(interior, here, axis=0, keepdims=False)
    for shift in range(1, ring):
        back = lax.dynamic_index_in_dim(interior, (here - shift) % ring, axis=0, keepdims=False)
        running = running + passed_along(back, "tq", -shift)
    return running[None]


def solution(mesh):
    tm_size = mesh.shape["tm"]
    lead_count = 4
    devices = mesh.devices.reshape(lead_count, tm_size // lead_count, mesh.shape["space"])
    ring_mesh = Mesh(devices, ("tq", "tr", "space"))
    tm = ("tq", "tr")
    in_specs = (
        P(tm, None, None, None, "space"),
        P(tm, "space", None, None),
        P(tm, "space"),
        P(tm, None, "space"),
        P(tm, None, "space"),
        P(tm, "space"),
    )
    out_specs = P(tm, None, None, "space")
    return jax.shard_map(body, mesh=ring_mesh, in_specs=in_specs, out_specs=out_specs, check_vma=False)
```

```python
import functools

import jax
import jax.numpy as jnp
from jax import lax
from jax.experimental import pallas as pl
from jax.experimental.pallas import tpu as pltpu
from jax.sharding import Mesh
from jax.sharding import PartitionSpec as P

GROUP_SITE_SPAN = 128
EDGE = 2
BLOCKS_PER_STEP = 32


def with_halo(block, sides, width):
    for axis, dim in sides:
        count = lax.axis_size(axis)
        forward = [(i, i + 1) for i in range(count - 1)]
        forward.append((count - 1, 0))
        backward = [(target, source) for source, target in forward]
        low = lax.ppermute(
            lax.slice_in_dim(block, block.shape[dim] - width, None, axis=dim), axis, forward
        )
        high = lax.ppermute(lax.slice_in_dim(block, 0, width, axis=dim), axis, backward)
        block = jnp.concatenate([low, block, high], axis=dim)
    return block


def passed_along(value, axis, steps):
    count = lax.axis_size(axis)
    pairs = [(source, (source + steps) % count) for source in range(count)]
    return lax.ppermute(value, axis, pairs)


def extend(grouped):
    return with_halo(grouped, (("space", grouped.ndim - 1),), EDGE * GROUP_SITE_SPAN)


def observe_kernel(idx_ref, cnt_ref, ext_ref, op_ref, val_ref, wt_ref, out_ref):
    step = pl.program_id(0)
    width = GROUP_SITE_SPAN
    fields = val_ref.shape[0]
    rows = ext_ref.shape[0]
    period = 8

    @pl.when(step == 0)
    def _():
        out_ref[...] = jnp.zeros_like(out_ref)

    count = cnt_ref[0]
    lane = lax.broadcasted_iota(jnp.int32, (1, width), 1)
    for k in range(BLOCKS_PER_STEP):
        b = step * BLOCKS_PER_STEP + k
        start = pl.multiple_of(idx_ref[b] * width, width)
        x = ext_ref[:, pl.ds(start, width)]
        op = op_ref[k]
        images = lax.dot_general(
            x, op, (((1,), (1,)), ((), ())), preferred_element_type=jnp.float32
        ).reshape(rows // period, period, width)
        observed = val_ref[:, k * width:(k + 1) * width].astype(jnp.float32)
        observed = jnp.concatenate([observed] * (period // fields), axis=0)[None]
        live = (b * width + lane) < count
        scaling = jnp.where(live, wt_ref[:, k * width:(k + 1) * width].astype(jnp.float32), 0.0)
        scaling = jnp.concatenate([scaling] * (period // fields), axis=0)[None]
        misfit = ((images - observed) * scaling).reshape(rows, width).astype(jnp.bfloat16)
        adjoint = jnp.dot(misfit, op, preferred_element_type=jnp.float32)
        out_ref[:, pl.ds(start, width)] += adjoint


def observe(ext_rows, operator, indices, values, weights, counts):
    rows, cells = ext_rows.shape
    obs_blocks = operator.shape[0]
    width = GROUP_SITE_SPAN
    fields = values.shape[0]
    steps = obs_blocks // BLOCKS_PER_STEP
    span = BLOCKS_PER_STEP * width
    grid_spec = pltpu.PrefetchScalarGridSpec(
        num_scalar_prefetch=2,
        grid=(steps,),
        in_specs=[
            pl.BlockSpec((rows, cells), lambda g, i, c: (0, 0)),
            pl.BlockSpec((BLOCKS_PER_STEP, width, width), lambda g, i, c: (g, 0, 0)),
            pl.BlockSpec((fields, span), lambda g, i, c: (0, g)),
            pl.BlockSpec((fields, span), lambda g, i, c: (0, g)),
        ],
        out_specs=pl.BlockSpec((rows, cells), lambda g, i, c: (0, 0)),
    )
    flops = 4 * obs_blocks * rows * width * width
    bytes_accessed = operator.size * 2 + ext_rows.size * 2 + rows * cells * 4 + values.size * 4
    return pl.pallas_call(
        observe_kernel,
        grid_spec=grid_spec,
        out_shape=jax.ShapeDtypeStruct((rows, cells), jnp.float32),
        compiler_params=pltpu.CompilerParams(dimension_semantics=("arbitrary",)),
        cost_estimate=pl.CostEstimate(
            flops=flops, bytes_accessed=bytes_accessed, transcendentals=0
        ),
    )(indices, counts, ext_rows, operator, values, weights)


def settle(adjoint_ext):
    rim_width = EDGE * GROUP_SITE_SPAN
    lower_rim = adjoint_ext[..., :rim_width]
    upper_rim = adjoint_ext[..., -rim_width:]
    interior = adjoint_ext[..., rim_width:-rim_width]
    from_above = passed_along(lower_rim, "space", -1)
    from_below = passed_along(upper_rim, "space", 1)
    interior = interior.at[..., -rim_width:].add(from_above)
    return interior.at[..., :rim_width].add(from_below)


def body(hindcast_archive, op_blocks, block_index, obs_values, obs_weights, obs_counts):
    ring = lax.axis_size("tq")
    here = lax.axis_index("tq")
    own = hindcast_archive[0]
    leads, members, fields, cells = own.shape
    own = own.reshape(leads, members * fields, cells)
    outgoing = jnp.roll(own, here, axis=0)
    incoming = lax.all_to_all(outgoing, "tq", 0, 0, tiled=True)
    extended = extend(incoming[None])[0]
    width = extended.shape[-1]
    adjoint_rows = observe(
        extended.reshape(leads * members * fields, width),
        op_blocks[0],
        block_index[0],
        obs_values[0],
        obs_weights[0],
        obs_counts[0],
    )
    interior = settle(adjoint_rows.reshape(1, leads, members * fields, width))[0]
    running = lax.dynamic_index_in_dim(interior, here, axis=0, keepdims=False)
    for shift in range(1, ring):
        back = lax.dynamic_index_in_dim(interior, (here - shift) % ring, axis=0, keepdims=False)
        running = running + passed_along(back, "tq", -shift)
    return running.reshape(1, members, fields, cells)


def solution(mesh):
    tm_size = mesh.shape["tm"]
    lead_count = 4
    devices = mesh.devices.reshape(lead_count, tm_size // lead_count, mesh.shape["space"])
    ring_mesh = Mesh(devices, ("tq", "tr", "space"))
    tm = ("tq", "tr")
    in_specs = (
        P(tm, None, None, None, "space"),
        P(tm, "space", None, None),
        P(tm, "space"),
        P(tm, None, "space"),
        P(tm, None, "space"),
        P(tm, "space"),
    )
    out_specs = P(tm, None, None, "space")
    return jax.shard_map(body, mesh=ring_mesh, in_specs=in_specs, out_specs=out_specs, check_vma=False)
```

```python
import functools

import jax
import jax.numpy as jnp
from jax import lax
from jax.experimental import pallas as pl
from jax.experimental.pallas import tpu as pltpu
from jax.sharding import Mesh
from jax.sharding import PartitionSpec as P

GROUP_SITE_SPAN = 128
EDGE = 2
BLOCKS_PER_STEP = 32


def with_halo(block, sides, width):
    for axis, dim in sides:
        count = lax.axis_size(axis)
        forward = [(i, i + 1) for i in range(count - 1)]
        forward.append((count - 1, 0))
        backward = [(target, source) for source, target in forward]
        low = lax.ppermute(
            lax.slice_in_dim(block, block.shape[dim] - width, None, axis=dim), axis, forward
        )
        high = lax.ppermute(lax.slice_in_dim(block, 0, width, axis=dim), axis, backward)
        block = jnp.concatenate([low, block, high], axis=dim)
    return block


def ring_pairs(count, steps):
    return [(source, (source + steps) % count) for source in range(count)]


def passed_along(value, axis, steps):
    count = lax.axis_size(axis)
    pairs = [(source, (source + steps) % count) for source in range(count)]
    return lax.ppermute(value, axis, pairs)


def extend(grouped):
    return with_halo(grouped, (("space", grouped.ndim - 1),), EDGE * GROUP_SITE_SPAN)


def observe_kernel(
    idx_ref, cnt_ref, low_ref, mid_ref, high_ref, op_ref, val_ref, wt_ref,
    low_out, mid_out, high_out, ext_ref, acc_ref,
):
    step = pl.program_id(0)
    width = GROUP_SITE_SPAN
    fields = val_ref.shape[0]
    rows = ext_ref.shape[0]
    rim = low_ref.shape[1]
    tile = mid_ref.shape[1]
    period = 8

    @pl.when(step == 0)
    def _():
        ext_ref[:, :rim] = low_ref[...]
        ext_ref[:, rim:rim + tile] = mid_ref[...]
        ext_ref[:, rim + tile:] = high_ref[...]
        acc_ref[...] = jnp.zeros_like(acc_ref)

    count = cnt_ref[0]
    lane = lax.broadcasted_iota(jnp.int32, (1, width), 1)
    for k in range(BLOCKS_PER_STEP):
        b = step * BLOCKS_PER_STEP + k
        start = pl.multiple_of(idx_ref[b] * width, width)
        x = ext_ref[:, pl.ds(start, width)]
        op = op_ref[k]
        images = lax.dot_general(
            x, op, (((1,), (1,)), ((), ())), preferred_element_type=jnp.float32
        ).reshape(rows // period, period, width)
        observed = val_ref[:, k * width:(k + 1) * width].astype(jnp.float32)
        observed = jnp.concatenate([observed] * (period // fields), axis=0)[None]
        live = (b * width + lane) < count
        scaling = jnp.where(live, wt_ref[:, k * width:(k + 1) * width].astype(jnp.float32), 0.0)
        scaling = jnp.concatenate([scaling] * (period // fields), axis=0)[None]
        misfit = ((images - observed) * scaling).reshape(rows, width).astype(jnp.bfloat16)
        adjoint = jnp.dot(misfit, op, preferred_element_type=jnp.float32)
        acc_ref[:, pl.ds(start, width)] += adjoint

    @pl.when(step == pl.num_programs(0) - 1)
    def _():
        low_out[...] = acc_ref[:, :rim]
        mid_out[...] = acc_ref[:, rim:rim + tile]
        high_out[...] = acc_ref[:, rim + tile:]


def observe(low, mid, high, operator, indices, values, weights, counts):
    rows, tile = mid.shape
    rim = low.shape[1]
    cells = tile + 2 * rim
    obs_blocks = operator.shape[0]
    width = GROUP_SITE_SPAN
    fields = values.shape[0]
    steps = obs_blocks // BLOCKS_PER_STEP
    span = BLOCKS_PER_STEP * width
    whole = lambda g, i, c: (0, 0)
    grid_spec = pltpu.PrefetchScalarGridSpec(
        num_scalar_prefetch=2,
        grid=(steps,),
        in_specs=[
            pl.BlockSpec((rows, rim), whole),
            pl.BlockSpec((rows, tile), whole),
            pl.BlockSpec((rows, rim), whole),
            pl.BlockSpec((BLOCKS_PER_STEP, width, width), lambda g, i, c: (g, 0, 0)),
            pl.BlockSpec((fields, span), lambda g, i, c: (0, g)),
            pl.BlockSpec((fields, span), lambda g, i, c: (0, g)),
        ],
        out_specs=[
            pl.BlockSpec((rows, rim), whole),
            pl.BlockSpec((rows, tile), whole),
            pl.BlockSpec((rows, rim), whole),
        ],
        scratch_shapes=[
            pltpu.VMEM((rows, cells), mid.dtype),
            pltpu.VMEM((rows, cells), jnp.float32),
        ],
    )
    flops = 4 * obs_blocks * rows * width * width
    bytes_accessed = operator.size * 2 + rows * cells * 6 + values.size * 4
    return pl.pallas_call(
        observe_kernel,
        grid_spec=grid_spec,
        out_shape=[
            jax.ShapeDtypeStruct((rows, rim), jnp.float32),
            jax.ShapeDtypeStruct((rows, tile), jnp.float32),
            jax.ShapeDtypeStruct((rows, rim), jnp.float32),
        ],
        compiler_params=pltpu.CompilerParams(dimension_semantics=("arbitrary",)),
        cost_estimate=pl.CostEstimate(
            flops=flops, bytes_accessed=bytes_accessed, transcendentals=0
        ),
    )(indices, counts, low, mid, high, operator, values, weights)


def settle(adjoint_ext):
    rim_width = EDGE * GROUP_SITE_SPAN
    lower_rim = adjoint_ext[..., :rim_width]
    upper_rim = adjoint_ext[..., -rim_width:]
    interior = adjoint_ext[..., rim_width:-rim_width]
    from_above = passed_along(lower_rim, "space", -1)
    from_below = passed_along(upper_rim, "space", 1)
    interior = interior.at[..., -rim_width:].add(from_above)
    return interior.at[..., :rim_width].add(from_below)


def body(hindcast_archive, op_blocks, block_index, obs_values, obs_weights, obs_counts):
    rim = EDGE * GROUP_SITE_SPAN
    space = lax.axis_size("space")
    ring = lax.axis_size("tq")
    here = lax.axis_index("tq")
    own = hindcast_archive[0]
    leads, members, fields, cells = own.shape
    rows = members * fields
    own = own.reshape(leads, rows, cells)
    outgoing = jnp.roll(own, here, axis=0)
    incoming = lax.all_to_all(outgoing, "tq", 0, 0, tiled=True)
    low = lax.ppermute(incoming[..., cells - rim:], "space", ring_pairs(space, 1))
    high = lax.ppermute(incoming[..., :rim], "space", ring_pairs(space, -1))
    low_adj, interior, high_adj = observe(
        low.reshape(leads * rows, rim),
        incoming.reshape(leads * rows, cells),
        high.reshape(leads * rows, rim),
        op_blocks[0],
        block_index[0],
        obs_values[0],
        obs_weights[0],
        obs_counts[0],
    )
    from_above = lax.ppermute(low_adj.reshape(leads, rows, rim), "space", ring_pairs(space, -1))
    from_below = lax.ppermute(high_adj.reshape(leads, rows, rim), "space", ring_pairs(space, 1))
    interior = interior.reshape(leads, rows, cells)
    interior = interior.at[..., cells - rim:].add(from_above)
    interior = interior.at[..., :rim].add(from_below)
    running = lax.dynamic_index_in_dim(interior, here, axis=0, keepdims=False)
    for shift in range(1, ring):
        back = lax.dynamic_index_in_dim(interior, (here - shift) % ring, axis=0, keepdims=False)
        running = running + passed_along(back, "tq", -shift)
    return running.reshape(1, members, fields, cells)


def solution(mesh):
    tm_size = mesh.shape["tm"]
    lead_count = 4
    devices = mesh.devices.reshape(lead_count, tm_size // lead_count, mesh.shape["space"])
    ring_mesh = Mesh(devices, ("tq", "tr", "space"))
    tm = ("tq", "tr")
    in_specs = (
        P(tm, None, None, None, "space"),
        P(tm, "space", None, None),
        P(tm, "space"),
        P(tm, None, "space"),
        P(tm, None, "space"),
        P(tm, "space"),
    )
    out_specs = P(tm, None, None, "space")
    return jax.shard_map(body, mesh=ring_mesh, in_specs=in_specs, out_specs=out_specs, check_vma=False)
```

```python
import functools

import jax
import jax.numpy as jnp
from jax import lax
from jax.experimental import pallas as pl
from jax.experimental.pallas import tpu as pltpu
from jax.sharding import Mesh
from jax.sharding import PartitionSpec as P

GROUP_SITE_SPAN = 128
EDGE = 2
BLOCKS_PER_STEP = 32


def with_halo(block, sides, width):
    for axis, dim in sides:
        count = lax.axis_size(axis)
        forward = [(i, i + 1) for i in range(count - 1)]
        forward.append((count - 1, 0))
        backward = [(target, source) for source, target in forward]
        low = lax.ppermute(
            lax.slice_in_dim(block, block.shape[dim] - width, None, axis=dim), axis, forward
        )
        high = lax.ppermute(lax.slice_in_dim(block, 0, width, axis=dim), axis, backward)
        block = jnp.concatenate([low, block, high], axis=dim)
    return block


def passed_along(value, axis, steps):
    count = lax.axis_size(axis)
    pairs = [(source, (source + steps) % count) for source in range(count)]
    return lax.ppermute(value, axis, pairs)


def extend(grouped):
    return with_halo(grouped, (("space", grouped.ndim - 1),), EDGE * GROUP_SITE_SPAN)


def observe_kernel(idx_ref, cnt_ref, ext_ref, op_ref, val_ref, wt_ref, out_ref):
    step = pl.program_id(0)
    width = GROUP_SITE_SPAN
    fields = val_ref.shape[0]
    rows = ext_ref.shape[0]
    period = 8

    @pl.when(step == 0)
    def _():
        out_ref[...] = jnp.zeros_like(out_ref)

    count = cnt_ref[0]
    lane = lax.broadcasted_iota(jnp.int32, (1, width), 1)
    for k in range(BLOCKS_PER_STEP):
        b = step * BLOCKS_PER_STEP + k
        start = pl.multiple_of(idx_ref[b] * width, width)
        x = ext_ref[:, pl.ds(start, width)]
        op = op_ref[k]
        images = lax.dot_general(
            x, op, (((1,), (1,)), ((), ())), preferred_element_type=jnp.float32
        ).reshape(rows // period, period, width)
        observed = val_ref[:, k * width:(k + 1) * width].astype(jnp.float32)
        observed = jnp.concatenate([observed] * (period // fields), axis=0)[None]
        live = (b * width + lane) < count
        scaling = jnp.where(live, wt_ref[:, k * width:(k + 1) * width].astype(jnp.float32), 0.0)
        scaling = jnp.concatenate([scaling] * (period // fields), axis=0)[None]
        misfit = ((images - observed) * scaling).reshape(rows, width).astype(jnp.bfloat16)
        adjoint = jnp.dot(misfit, op, preferred_element_type=jnp.float32)
        out_ref[:, pl.ds(start, width)] += adjoint


def observe(ext_rows, operator, indices, values, weights, counts):
    rows, cells = ext_rows.shape
    obs_blocks = operator.shape[0]
    width = GROUP_SITE_SPAN
    fields = values.shape[0]
    steps = obs_blocks // BLOCKS_PER_STEP
    span = BLOCKS_PER_STEP * width
    grid_spec = pltpu.PrefetchScalarGridSpec(
        num_scalar_prefetch=2,
        grid=(steps,),
        in_specs=[
            pl.BlockSpec((rows, cells), lambda g, i, c: (0, 0)),
            pl.BlockSpec((BLOCKS_PER_STEP, width, width), lambda g, i, c: (g, 0, 0)),
            pl.BlockSpec((fields, span), lambda g, i, c: (0, g)),
            pl.BlockSpec((fields, span), lambda g, i, c: (0, g)),
        ],
        out_specs=pl.BlockSpec((rows, cells), lambda g, i, c: (0, 0)),
    )
    flops = 4 * obs_blocks * rows * width * width
    bytes_accessed = operator.size * 2 + ext_rows.size * 2 + rows * cells * 4 + values.size * 4
    return pl.pallas_call(
        observe_kernel,
        grid_spec=grid_spec,
        out_shape=jax.ShapeDtypeStruct((rows, cells), jnp.float32),
        compiler_params=pltpu.CompilerParams(dimension_semantics=("arbitrary",)),
        cost_estimate=pl.CostEstimate(
            flops=flops, bytes_accessed=bytes_accessed, transcendentals=0
        ),
    )(indices, counts, ext_rows, operator, values, weights)


def settle(adjoint_ext):
    rim_width = EDGE * GROUP_SITE_SPAN
    lower_rim = adjoint_ext[..., :rim_width]
    upper_rim = adjoint_ext[..., -rim_width:]
    interior = adjoint_ext[..., rim_width:-rim_width]
    from_above = passed_along(lower_rim, "space", -1)
    from_below = passed_along(upper_rim, "space", 1)
    interior = interior.at[..., -rim_width:].add(from_above)
    return interior.at[..., :rim_width].add(from_below)


def body(hindcast_archive, op_blocks, block_index, obs_values, obs_weights, obs_counts):
    ring = lax.axis_size("tq")
    here = lax.axis_index("tq")
    own = hindcast_archive[0]
    leads, members, fields, cells = own.shape
    own = own.reshape(leads, members * fields, cells)
    outgoing = jnp.roll(own, here, axis=0)
    incoming = lax.all_to_all(outgoing, "tq", 0, 0, tiled=True)
    extended = extend(incoming[None])[0]
    width = extended.shape[-1]
    adjoint_rows = observe(
        extended.reshape(leads * members * fields, width),
        op_blocks[0],
        block_index[0],
        obs_values[0],
        obs_weights[0],
        obs_counts[0],
    )
    interior = settle(adjoint_rows.reshape(1, leads, members * fields, width))[0]
    running = lax.dynamic_index_in_dim(interior, here, axis=0, keepdims=False)
    for shift in sorted(range(1, ring), key=lambda d: -min(d, ring - d)):
        back = lax.dynamic_index_in_dim(interior, (here - shift) % ring, axis=0, keepdims=False)
        running = running + passed_along(back, "tq", -shift)
    return running.reshape(1, members, fields, cells)


def solution(mesh):
    tm_size = mesh.shape["tm"]
    lead_count = 4
    devices = mesh.devices.reshape(lead_count, tm_size // lead_count, mesh.shape["space"])
    ring_mesh = Mesh(devices, ("tq", "tr", "space"))
    tm = ("tq", "tr")
    in_specs = (
        P(tm, None, None, None, "space"),
        P(tm, "space", None, None),
        P(tm, "space"),
        P(tm, None, "space"),
        P(tm, None, "space"),
        P(tm, "space"),
    )
    out_specs = P(tm, None, None, "space")
    return jax.shard_map(body, mesh=ring_mesh, in_specs=in_specs, out_specs=out_specs, check_vma=False)
```

```python
import functools

import jax
import jax.numpy as jnp
from jax import lax
from jax.experimental import pallas as pl
from jax.experimental.pallas import tpu as pltpu
from jax.sharding import Mesh
from jax.sharding import PartitionSpec as P

GROUP_SITE_SPAN = 128
EDGE = 2
BLOCKS_PER_STEP = 32


def with_halo(block, sides, width):
    for axis, dim in sides:
        count = lax.axis_size(axis)
        forward = [(i, i + 1) for i in range(count - 1)]
        forward.append((count - 1, 0))
        backward = [(target, source) for source, target in forward]
        low = lax.ppermute(
            lax.slice_in_dim(block, block.shape[dim] - width, None, axis=dim), axis, forward
        )
        high = lax.ppermute(lax.slice_in_dim(block, 0, width, axis=dim), axis, backward)
        block = jnp.concatenate([low, block, high], axis=dim)
    return block


def passed_along(value, axis, steps):
    count = lax.axis_size(axis)
    pairs = [(source, (source + steps) % count) for source in range(count)]
    return lax.ppermute(value, axis, pairs)


def extend(grouped):
    return with_halo(grouped, (("space", grouped.ndim - 1),), EDGE * GROUP_SITE_SPAN)


def observe_kernel(idx_ref, cnt_ref, ext_ref, op_ref, val_ref, wt_ref, out_ref):
    step = pl.program_id(0)
    width = GROUP_SITE_SPAN
    fields = val_ref.shape[0]
    rows = ext_ref.shape[0]
    period = 8

    @pl.when(step == 0)
    def _():
        out_ref[...] = jnp.zeros_like(out_ref)

    count = cnt_ref[0]
    lane = lax.broadcasted_iota(jnp.int32, (1, width), 1)
    for k in range(BLOCKS_PER_STEP):
        b = step * BLOCKS_PER_STEP + k
        start = pl.multiple_of(idx_ref[b] * width, width)
        x = ext_ref[:, pl.ds(start, width)]
        op = op_ref[k]
        images = lax.dot_general(
            x, op, (((1,), (1,)), ((), ())), preferred_element_type=jnp.float32
        ).reshape(rows // period, period, width)
        observed = val_ref[:, k * width:(k + 1) * width].astype(jnp.float32)
        observed = jnp.concatenate([observed] * (period // fields), axis=0)[None]
        live = (b * width + lane) < count
        scaling = jnp.where(live, wt_ref[:, k * width:(k + 1) * width].astype(jnp.float32), 0.0)
        scaling = jnp.concatenate([scaling] * (period // fields), axis=0)[None]
        misfit = ((images - observed) * scaling).reshape(rows, width).astype(jnp.bfloat16)
        adjoint = jnp.dot(misfit, op, preferred_element_type=jnp.float32)
        out_ref[:, pl.ds(start, width)] += adjoint


def observe(ext_rows, operator, indices, values, weights, counts):
    rows, cells = ext_rows.shape
    obs_blocks = operator.shape[0]
    width = GROUP_SITE_SPAN
    fields = values.shape[0]
    steps = obs_blocks // BLOCKS_PER_STEP
    span = BLOCKS_PER_STEP * width
    grid_spec = pltpu.PrefetchScalarGridSpec(
        num_scalar_prefetch=2,
        grid=(steps,),
        in_specs=[
            pl.BlockSpec((rows, cells), lambda g, i, c: (0, 0)),
            pl.BlockSpec((BLOCKS_PER_STEP, width, width), lambda g, i, c: (g, 0, 0)),
            pl.BlockSpec((fields, span), lambda g, i, c: (0, g)),
            pl.BlockSpec((fields, span), lambda g, i, c: (0, g)),
        ],
        out_specs=pl.BlockSpec((rows, cells), lambda g, i, c: (0, 0)),
    )
    flops = 4 * obs_blocks * rows * width * width
    bytes_accessed = operator.size * 2 + ext_rows.size * 2 + rows * cells * 4 + values.size * 4
    return pl.pallas_call(
        observe_kernel,
        grid_spec=grid_spec,
        out_shape=jax.ShapeDtypeStruct((rows, cells), jnp.float32),
        compiler_params=pltpu.CompilerParams(dimension_semantics=("arbitrary",)),
        cost_estimate=pl.CostEstimate(
            flops=flops, bytes_accessed=bytes_accessed, transcendentals=0
        ),
    )(indices, counts, ext_rows, operator, values, weights)


def settle(adjoint_ext):
    rim_width = EDGE * GROUP_SITE_SPAN
    lower_rim = adjoint_ext[..., :rim_width]
    upper_rim = adjoint_ext[..., -rim_width:]
    interior = adjoint_ext[..., rim_width:-rim_width]
    from_above = passed_along(lower_rim, "space", -1)
    from_below = passed_along(upper_rim, "space", 1)
    interior = interior.at[..., -rim_width:].add(from_above)
    return interior.at[..., :rim_width].add(from_below)


def body(hindcast_archive, op_blocks, block_index, obs_values, obs_weights, obs_counts):
    ring = lax.axis_size("tq")
    here = lax.axis_index("tq")
    own = hindcast_archive[0]
    leads, members, fields, cells = own.shape
    own = own.reshape(leads, members * fields, cells)
    outgoing = jnp.roll(own, here, axis=0)
    incoming = lax.all_to_all(outgoing, "tq", 0, 0, tiled=True)
    extended = extend(incoming[None])[0]
    width = extended.shape[-1]
    adjoint_rows = observe(
        extended.reshape(leads * members * fields, width),
        op_blocks[0],
        block_index[0],
        obs_values[0],
        obs_weights[0],
        obs_counts[0],
    )
    interior = settle(adjoint_rows.reshape(1, leads, members * fields, width))[0]
    returned = lax.all_to_all(interior, "tq", 0, 0, tiled=True)
    running = returned[0]
    for slot in range(1, ring):
        running = running + returned[slot]
    return running.reshape(1, members, fields, cells)


def solution(mesh):
    tm_size = mesh.shape["tm"]
    lead_count = 4
    devices = mesh.devices.reshape(lead_count, tm_size // lead_count, mesh.shape["space"])
    ring_mesh = Mesh(devices, ("tq", "tr", "space"))
    tm = ("tq", "tr")
    in_specs = (
        P(tm, None, None, None, "space"),
        P(tm, "space", None, None),
        P(tm, "space"),
        P(tm, None, "space"),
        P(tm, None, "space"),
        P(tm, "space"),
    )
    out_specs = P(tm, None, None, "space")
    return jax.shard_map(body, mesh=ring_mesh, in_specs=in_specs, out_specs=out_specs, check_vma=False)
```

```python
import functools

import jax
import jax.numpy as jnp
from jax import lax
from jax.experimental import pallas as pl
from jax.experimental.pallas import tpu as pltpu
from jax.sharding import Mesh
from jax.sharding import PartitionSpec as P

GROUP_SITE_SPAN = 128
EDGE = 2
BLOCKS_PER_STEP = 96


def with_halo(block, sides, width):
    for axis, dim in sides:
        count = lax.axis_size(axis)
        forward = [(i, i + 1) for i in range(count - 1)]
        forward.append((count - 1, 0))
        backward = [(target, source) for source, target in forward]
        low = lax.ppermute(
            lax.slice_in_dim(block, block.shape[dim] - width, None, axis=dim), axis, forward
        )
        high = lax.ppermute(lax.slice_in_dim(block, 0, width, axis=dim), axis, backward)
        block = jnp.concatenate([low, block, high], axis=dim)
    return block


def ring_pairs(count, steps):
    return [(source, (source + steps) % count) for source in range(count)]


def passed_along(value, axis, steps):
    count = lax.axis_size(axis)
    pairs = [(source, (source + steps) % count) for source in range(count)]
    return lax.ppermute(value, axis, pairs)


def extend(grouped):
    return with_halo(grouped, (("space", grouped.ndim - 1),), EDGE * GROUP_SITE_SPAN)


def observe_kernel(idx_ref, cnt_ref, low_ref, mid_ref, high_ref, op_ref, val_ref, wt_ref, out_ref, ext_ref):
    step = pl.program_id(0)
    width = GROUP_SITE_SPAN
    fields = val_ref.shape[0]
    rows = ext_ref.shape[0]
    rim = low_ref.shape[1]
    tile = mid_ref.shape[1]
    blocks = op_ref.shape[0]
    period = 8

    @pl.when(step == 0)
    def _():
        ext_ref[:, :rim] = low_ref[...]
        ext_ref[:, rim:rim + tile] = mid_ref[...]
        ext_ref[:, rim + tile:] = high_ref[...]
        out_ref[...] = jnp.zeros_like(out_ref)

    count = cnt_ref[0]
    lane = lax.broadcasted_iota(jnp.int32, (1, width), 1)

    def forward(k):
        b = step * blocks + k
        start = pl.multiple_of(idx_ref[b] * width, width)
        x = ext_ref[:, pl.ds(start, width)]
        op = op_ref[k]
        images = lax.dot_general(
            x, op, (((1,), (1,)), ((), ())), preferred_element_type=jnp.float32
        ).reshape(rows // period, period, width)
        observed = val_ref[:, k * width:(k + 1) * width].astype(jnp.float32)
        observed = jnp.concatenate([observed] * (period // fields), axis=0)[None]
        live = (b * width + lane) < count
        scaling = jnp.where(live, wt_ref[:, k * width:(k + 1) * width].astype(jnp.float32), 0.0)
        scaling = jnp.concatenate([scaling] * (period // fields), axis=0)[None]
        misfit = ((images - observed) * scaling).reshape(rows, width).astype(jnp.bfloat16)
        return start, misfit, op

    def backward(start, misfit, op):
        out_ref[:, pl.ds(start, width)] += jnp.dot(misfit, op, preferred_element_type=jnp.float32)

    pending = forward(0)
    for k in range(1, blocks):
        ahead = forward(k)
        backward(*pending)
        pending = ahead
    backward(*pending)


def observe(low, mid, high, operator, indices, values, weights, counts):
    rows, tile = mid.shape
    rim = low.shape[1]
    cells = tile + 2 * rim
    obs_blocks = operator.shape[0]
    width = GROUP_SITE_SPAN
    fields = values.shape[0]
    steps = obs_blocks // BLOCKS_PER_STEP
    span = BLOCKS_PER_STEP * width
    whole = lambda g, i, c: (0, 0)
    grid_spec = pltpu.PrefetchScalarGridSpec(
        num_scalar_prefetch=2,
        grid=(steps,),
        in_specs=[
            pl.BlockSpec((rows, rim), whole),
            pl.BlockSpec((rows, tile), whole),
            pl.BlockSpec((rows, rim), whole),
            pl.BlockSpec((BLOCKS_PER_STEP, width, width), lambda g, i, c: (g, 0, 0)),
            pl.BlockSpec((fields, span), lambda g, i, c: (0, g)),
            pl.BlockSpec((fields, span), lambda g, i, c: (0, g)),
        ],
        out_specs=pl.BlockSpec((rows, cells), whole),
        scratch_shapes=[pltpu.VMEM((rows, cells), mid.dtype)],
    )
    flops = 4 * obs_blocks * rows * width * width
    bytes_accessed = operator.size * 2 + rows * cells * 6 + values.size * 4
    return pl.pallas_call(
        observe_kernel,
        grid_spec=grid_spec,
        out_shape=jax.ShapeDtypeStruct((rows, cells), jnp.float32),
        compiler_params=pltpu.CompilerParams(dimension_semantics=("arbitrary",)),
        cost_estimate=pl.CostEstimate(
            flops=flops, bytes_accessed=bytes_accessed, transcendentals=0
        ),
    )(indices, counts, low, mid, high, operator, values, weights)


def settle(adjoint_ext):
    rim_width = EDGE * GROUP_SITE_SPAN
    lower_rim = adjoint_ext[..., :rim_width]
    upper_rim = adjoint_ext[..., -rim_width:]
    interior = adjoint_ext[..., rim_width:-rim_width]
    from_above = passed_along(lower_rim, "space", -1)
    from_below = passed_along(upper_rim, "space", 1)
    interior = interior.at[..., -rim_width:].add(from_above)
    return interior.at[..., :rim_width].add(from_below)


def body(hindcast_archive, op_blocks, block_index, obs_values, obs_weights, obs_counts):
    ring = lax.axis_size("tq")
    here = lax.axis_index("tq")
    own = hindcast_archive[0]
    leads, members, fields, cells = own.shape
    own = own.reshape(leads, members * fields, cells)
    outgoing = jnp.roll(own, here, axis=0)
    incoming = lax.all_to_all(outgoing, "tq", 0, 0, tiled=True)
    rim = EDGE * GROUP_SITE_SPAN
    space = lax.axis_size("space")
    low = lax.ppermute(incoming[..., cells - rim:], "space", ring_pairs(space, 1))
    high = lax.ppermute(incoming[..., :rim], "space", ring_pairs(space, -1))
    width = cells + 2 * rim
    adjoint_rows = observe(
        low.reshape(leads * members * fields, rim),
        incoming.reshape(leads * members * fields, cells),
        high.reshape(leads * members * fields, rim),
        op_blocks[0],
        block_index[0],
        obs_values[0],
        obs_weights[0],
        obs_counts[0],
    )
    interior = settle(adjoint_rows.reshape(1, leads, members * fields, width))[0]
    returned = lax.all_to_all(interior, "tq", 0, 0, tiled=True)
    running = returned[0]
    for slot in range(1, ring):
        running = running + returned[slot]
    return running.reshape(1, members, fields, cells)


def solution(mesh):
    tm_size = mesh.shape["tm"]
    lead_count = 4
    devices = mesh.devices.reshape(lead_count, tm_size // lead_count, mesh.shape["space"])
    ring_mesh = Mesh(devices, ("tq", "tr", "space"))
    tm = ("tq", "tr")
    in_specs = (
        P(tm, None, None, None, "space"),
        P(tm, "space", None, None),
        P(tm, "space"),
        P(tm, None, "space"),
        P(tm, None, "space"),
        P(tm, "space"),
    )
    out_specs = P(tm, None, None, "space")
    return jax.shard_map(body, mesh=ring_mesh, in_specs=in_specs, out_specs=out_specs, check_vma=False)
```

```python
import functools

import jax
import jax.numpy as jnp
from jax import lax
from jax.experimental import pallas as pl
from jax.experimental.pallas import tpu as pltpu
from jax.sharding import Mesh
from jax.sharding import PartitionSpec as P

GROUP_SITE_SPAN = 128
EDGE = 2
BLOCKS_PER_STEP = 96


def with_halo(block, sides, width):
    for axis, dim in sides:
        count = lax.axis_size(axis)
        forward = [(i, i + 1) for i in range(count - 1)]
        forward.append((count - 1, 0))
        backward = [(target, source) for source, target in forward]
        low = lax.ppermute(
            lax.slice_in_dim(block, block.shape[dim] - width, None, axis=dim), axis, forward
        )
        high = lax.ppermute(lax.slice_in_dim(block, 0, width, axis=dim), axis, backward)
        block = jnp.concatenate([low, block, high], axis=dim)
    return block


def ring_pairs(count, steps):
    return [(source, (source + steps) % count) for source in range(count)]


def passed_along(value, axis, steps):
    count = lax.axis_size(axis)
    pairs = [(source, (source + steps) % count) for source in range(count)]
    return lax.ppermute(value, axis, pairs)


def extend(grouped):
    return with_halo(grouped, (("space", grouped.ndim - 1),), EDGE * GROUP_SITE_SPAN)


def observe_kernel(
    idx_ref, cnt_ref, low_ref, mid_ref, high_ref, op_ref, val_ref, wt_ref,
    low_out, mid_out, high_out, ext_ref, out_ref,
):
    step = pl.program_id(0)
    width = GROUP_SITE_SPAN
    fields = val_ref.shape[0]
    rows = ext_ref.shape[0]
    rim = low_ref.shape[1]
    tile = mid_ref.shape[1]
    blocks = op_ref.shape[0]
    period = 8

    @pl.when(step == 0)
    def _():
        ext_ref[:, :rim] = low_ref[...]
        ext_ref[:, rim:rim + tile] = mid_ref[...]
        ext_ref[:, rim + tile:] = high_ref[...]
        out_ref[...] = jnp.zeros_like(out_ref)

    count = cnt_ref[0]
    lane = lax.broadcasted_iota(jnp.int32, (1, width), 1)

    def forward(k):
        b = step * blocks + k
        start = pl.multiple_of(idx_ref[b] * width, width)
        x = ext_ref[:, pl.ds(start, width)]
        op = op_ref[k]
        images = lax.dot_general(
            x, op, (((1,), (1,)), ((), ())), preferred_element_type=jnp.float32
        ).reshape(rows // period, period, width)
        observed = val_ref[:, k * width:(k + 1) * width].astype(jnp.float32)
        observed = jnp.concatenate([observed] * (period // fields), axis=0)[None]
        live = (b * width + lane) < count
        scaling = jnp.where(live, wt_ref[:, k * width:(k + 1) * width].astype(jnp.float32), 0.0)
        scaling = jnp.concatenate([scaling] * (period // fields), axis=0)[None]
        misfit = ((images - observed) * scaling).reshape(rows, width).astype(jnp.bfloat16)
        return start, misfit, op

    def backward(start, misfit, op):
        out_ref[:, pl.ds(start, width)] += jnp.dot(misfit, op, preferred_element_type=jnp.float32)

    pending = forward(0)
    for k in range(1, blocks):
        ahead = forward(k)
        backward(*pending)
        pending = ahead
    backward(*pending)

    @pl.when(step == pl.num_programs(0) - 1)
    def _():
        low_out[...] = out_ref[:, :rim]
        mid_out[...] = out_ref[:, rim:rim + tile]
        high_out[...] = out_ref[:, rim + tile:]


def observe(low, mid, high, operator, indices, values, weights, counts):
    rows, tile = mid.shape
    rim = low.shape[1]
    cells = tile + 2 * rim
    obs_blocks = operator.shape[0]
    width = GROUP_SITE_SPAN
    fields = values.shape[0]
    steps = obs_blocks // BLOCKS_PER_STEP
    span = BLOCKS_PER_STEP * width
    whole = lambda g, i, c: (0, 0)
    grid_spec = pltpu.PrefetchScalarGridSpec(
        num_scalar_prefetch=2,
        grid=(steps,),
        in_specs=[
            pl.BlockSpec((rows, rim), whole),
            pl.BlockSpec((rows, tile), whole),
            pl.BlockSpec((rows, rim), whole),
            pl.BlockSpec((BLOCKS_PER_STEP, width, width), lambda g, i, c: (g, 0, 0)),
            pl.BlockSpec((fields, span), lambda g, i, c: (0, g)),
            pl.BlockSpec((fields, span), lambda g, i, c: (0, g)),
        ],
        out_specs=[
            pl.BlockSpec((rows, rim), whole),
            pl.BlockSpec((rows, tile), whole),
            pl.BlockSpec((rows, rim), whole),
        ],
        scratch_shapes=[
            pltpu.VMEM((rows, cells), mid.dtype),
            pltpu.VMEM((rows, cells), jnp.float32),
        ],
    )
    flops = 4 * obs_blocks * rows * width * width
    bytes_accessed = operator.size * 2 + rows * cells * 6 + values.size * 4
    return pl.pallas_call(
        observe_kernel,
        grid_spec=grid_spec,
        out_shape=[
            jax.ShapeDtypeStruct((rows, rim), jnp.float32),
            jax.ShapeDtypeStruct((rows, tile), jnp.float32),
            jax.ShapeDtypeStruct((rows, rim), jnp.float32),
        ],
        compiler_params=pltpu.CompilerParams(dimension_semantics=("arbitrary",)),
        cost_estimate=pl.CostEstimate(
            flops=flops, bytes_accessed=bytes_accessed, transcendentals=0
        ),
    )(indices, counts, low, mid, high, operator, values, weights)


def rim_kernel(below_ref, above_ref, edge_ref, out_ref):
    side = pl.program_id(0)

    @pl.when(side == 0)
    def _():
        out_ref[...] = edge_ref[...] + below_ref[...]

    @pl.when(side == 1)
    def _():
        out_ref[...] = edge_ref[...] + above_ref[...]


def add_rims(interior, from_below, from_above):
    rows, tile = interior.shape
    rim = from_below.shape[1]
    last = tile // rim - 1
    edge = pl.BlockSpec((rows, rim), lambda side: (0, side * last))
    whole = pl.BlockSpec((rows, rim), lambda side: (0, 0))
    return pl.pallas_call(
        rim_kernel,
        grid=(2,),
        in_specs=[whole, whole, edge],
        out_specs=edge,
        out_shape=jax.ShapeDtypeStruct(interior.shape, interior.dtype),
        input_output_aliases={2: 0},
        compiler_params=pltpu.CompilerParams(dimension_semantics=("arbitrary",)),
    )(from_below, from_above, interior)


def settle(adjoint_ext):
    rim_width = EDGE * GROUP_SITE_SPAN
    lower_rim = adjoint_ext[..., :rim_width]
    upper_rim = adjoint_ext[..., -rim_width:]
    interior = adjoint_ext[..., rim_width:-rim_width]
    from_above = passed_along(lower_rim, "space", -1)
    from_below = passed_along(upper_rim, "space", 1)
    interior = interior.at[..., -rim_width:].add(from_above)
    return interior.at[..., :rim_width].add(from_below)


def body(hindcast_archive, op_blocks, block_index, obs_values, obs_weights, obs_counts):
    ring = lax.axis_size("tq")
    here = lax.axis_index("tq")
    own = hindcast_archive[0]
    leads, members, fields, cells = own.shape
    own = own.reshape(leads, members * fields, cells)
    outgoing = jnp.roll(own, here, axis=0)
    incoming = lax.all_to_all(outgoing, "tq", 0, 0, tiled=True)
    rim = EDGE * GROUP_SITE_SPAN
    space = lax.axis_size("space")
    low = lax.ppermute(incoming[..., cells - rim:], "space", ring_pairs(space, 1))
    high = lax.ppermute(incoming[..., :rim], "space", ring_pairs(space, -1))
    rows = leads * members * fields
    low_adj, interior, high_adj = observe(
        low.reshape(rows, rim),
        incoming.reshape(rows, cells),
        high.reshape(rows, rim),
        op_blocks[0],
        block_index[0],
        obs_values[0],
        obs_weights[0],
        obs_counts[0],
    )
    from_above = lax.ppermute(low_adj, "space", ring_pairs(space, -1))
    from_below = lax.ppermute(high_adj, "space", ring_pairs(space, 1))
    interior = add_rims(interior, from_below, from_above).reshape(leads, members * fields, cells)
    returned = lax.all_to_all(interior, "tq", 0, 0, tiled=True)
    running = returned[0]
    for slot in range(1, ring):
        running = running + returned[slot]
    return running.reshape(1, members, fields, cells)


def solution(mesh):
    tm_size = mesh.shape["tm"]
    lead_count = 4
    devices = mesh.devices.reshape(lead_count, tm_size // lead_count, mesh.shape["space"])
    ring_mesh = Mesh(devices, ("tq", "tr", "space"))
    tm = ("tq", "tr")
    in_specs = (
        P(tm, None, None, None, "space"),
        P(tm, "space", None, None),
        P(tm, "space"),
        P(tm, None, "space"),
        P(tm, None, "space"),
        P(tm, "space"),
    )
    out_specs = P(tm, None, None, "space")
    return jax.shard_map(body, mesh=ring_mesh, in_specs=in_specs, out_specs=out_specs, check_vma=False)
```

```python
import functools

import jax
import jax.numpy as jnp
from jax import lax
from jax.experimental import pallas as pl
from jax.experimental.pallas import tpu as pltpu
from jax.sharding import Mesh
from jax.sharding import PartitionSpec as P

GROUP_SITE_SPAN = 128
EDGE = 2
BLOCKS_PER_STEP = 96


def with_halo(block, sides, width):
    for axis, dim in sides:
        count = lax.axis_size(axis)
        forward = [(i, i + 1) for i in range(count - 1)]
        forward.append((count - 1, 0))
        backward = [(target, source) for source, target in forward]
        low = lax.ppermute(
            lax.slice_in_dim(block, block.shape[dim] - width, None, axis=dim), axis, forward
        )
        high = lax.ppermute(lax.slice_in_dim(block, 0, width, axis=dim), axis, backward)
        block = jnp.concatenate([low, block, high], axis=dim)
    return block


def ring_pairs(count, steps):
    return [(source, (source + steps) % count) for source in range(count)]


def passed_along(value, axis, steps):
    count = lax.axis_size(axis)
    pairs = [(source, (source + steps) % count) for source in range(count)]
    return lax.ppermute(value, axis, pairs)


def extend(grouped):
    return with_halo(grouped, (("space", grouped.ndim - 1),), EDGE * GROUP_SITE_SPAN)


def observe_kernel(idx_ref, cnt_ref, ext_ref, op_ref, val_ref, wt_ref, out_ref):
    step = pl.program_id(0)
    width = GROUP_SITE_SPAN
    fields = val_ref.shape[0]
    rows = ext_ref.shape[0]
    blocks = op_ref.shape[0]
    period = 8

    @pl.when(step == 0)
    def _():
        out_ref[...] = jnp.zeros_like(out_ref)

    count = cnt_ref[0]
    lane = lax.broadcasted_iota(jnp.int32, (1, width), 1)

    def forward(k):
        b = step * blocks + k
        start = pl.multiple_of(idx_ref[b] * width, width)
        x = ext_ref[:, pl.ds(start, width)]
        op = op_ref[k]
        images = lax.dot_general(
            x, op, (((1,), (1,)), ((), ())), preferred_element_type=jnp.float32
        ).reshape(rows // period, period, width)
        observed = val_ref[:, k * width:(k + 1) * width].astype(jnp.float32)
        observed = jnp.concatenate([observed] * (period // fields), axis=0)[None]
        live = (b * width + lane) < count
        scaling = jnp.where(live, wt_ref[:, k * width:(k + 1) * width].astype(jnp.float32), 0.0)
        scaling = jnp.concatenate([scaling] * (period // fields), axis=0)[None]
        misfit = ((images - observed) * scaling).reshape(rows, width).astype(jnp.bfloat16)
        return start, misfit, op

    def backward(start, misfit, op):
        out_ref[:, pl.ds(start, width)] += jnp.dot(misfit, op, preferred_element_type=jnp.float32)

    pending = forward(0)
    for k in range(1, blocks):
        ahead = forward(k)
        backward(*pending)
        pending = ahead
    backward(*pending)


def observe(ext_rows, operator, indices, values, weights, counts):
    rows, cells = ext_rows.shape
    obs_blocks = operator.shape[0]
    width = GROUP_SITE_SPAN
    fields = values.shape[0]
    steps = obs_blocks // BLOCKS_PER_STEP
    span = BLOCKS_PER_STEP * width
    whole = lambda g, i, c: (0, 0)
    grid_spec = pltpu.PrefetchScalarGridSpec(
        num_scalar_prefetch=2,
        grid=(steps,),
        in_specs=[
            pl.BlockSpec((rows, cells), whole),
            pl.BlockSpec((BLOCKS_PER_STEP, width, width), lambda g, i, c: (g, 0, 0)),
            pl.BlockSpec((fields, span), lambda g, i, c: (0, g)),
            pl.BlockSpec((fields, span), lambda g, i, c: (0, g)),
        ],
        out_specs=pl.BlockSpec((rows, cells), whole),
    )
    flops = 4 * obs_blocks * rows * width * width
    bytes_accessed = operator.size * 2 + rows * cells * 6 + values.size * 4
    return pl.pallas_call(
        observe_kernel,
        grid_spec=grid_spec,
        out_shape=jax.ShapeDtypeStruct((rows, cells), jnp.float32),
        compiler_params=pltpu.CompilerParams(dimension_semantics=("arbitrary",)),
        cost_estimate=pl.CostEstimate(
            flops=flops, bytes_accessed=bytes_accessed, transcendentals=0
        ),
    )(indices, counts, ext_rows, operator, values, weights)


def settle(adjoint_ext):
    rim_width = EDGE * GROUP_SITE_SPAN
    lower_rim = adjoint_ext[..., :rim_width]
    upper_rim = adjoint_ext[..., -rim_width:]
    interior = adjoint_ext[..., rim_width:-rim_width]
    from_above = passed_along(lower_rim, "space", -1)
    from_below = passed_along(upper_rim, "space", 1)
    interior = interior.at[..., -rim_width:].add(from_above)
    return interior.at[..., :rim_width].add(from_below)


def body(hindcast_archive, op_blocks, block_index, obs_values, obs_weights, obs_counts):
    ring = lax.axis_size("tq")
    here = lax.axis_index("tq")
    own = hindcast_archive[0]
    leads, members, fields, cells = own.shape
    own = own.reshape(leads, members * fields, cells)
    rim = EDGE * GROUP_SITE_SPAN
    space = lax.axis_size("space")
    low = lax.ppermute(own[..., cells - rim:], "space", ring_pairs(space, 1))
    high = lax.ppermute(own[..., :rim], "space", ring_pairs(space, -1))
    extended = jnp.concatenate([low, own, high], axis=-1)
    outgoing = jnp.roll(extended, here, axis=0)
    incoming = lax.all_to_all(outgoing, "tq", 0, 0, tiled=True)
    width = cells + 2 * rim
    adjoint_rows = observe(
        incoming.reshape(leads * members * fields, width),
        op_blocks[0],
        block_index[0],
        obs_values[0],
        obs_weights[0],
        obs_counts[0],
    )
    interior = settle(adjoint_rows.reshape(1, leads, members * fields, width))[0]
    returned = lax.all_to_all(interior, "tq", 0, 0, tiled=True)
    running = returned[0]
    for slot in range(1, ring):
        running = running + returned[slot]
    return running.reshape(1, members, fields, cells)


def solution(mesh):
    tm_size = mesh.shape["tm"]
    lead_count = 4
    devices = mesh.devices.reshape(lead_count, tm_size // lead_count, mesh.shape["space"])
    ring_mesh = Mesh(devices, ("tq", "tr", "space"))
    tm = ("tq", "tr")
    in_specs = (
        P(tm, None, None, None, "space"),
        P(tm, "space", None, None),
        P(tm, "space"),
        P(tm, None, "space"),
        P(tm, None, "space"),
        P(tm, "space"),
    )
    out_specs = P(tm, None, None, "space")
    return jax.shard_map(body, mesh=ring_mesh, in_specs=in_specs, out_specs=out_specs, check_vma=False)
```

```python
import functools

import functools

import jax
import jax.numpy as jnp
from jax import lax
from jax.experimental import pallas as pl
from jax.experimental.pallas import tpu as pltpu
from jax.sharding import Mesh
from jax.sharding import PartitionSpec as P

GROUP_SITE_SPAN = 128
EDGE = 2
BLOCKS_PER_STEP = 96


def with_halo(block, sides, width):
    for axis, dim in sides:
        count = lax.axis_size(axis)
        forward = [(i, i + 1) for i in range(count - 1)]
        forward.append((count - 1, 0))
        backward = [(target, source) for source, target in forward]
        low = lax.ppermute(
            lax.slice_in_dim(block, block.shape[dim] - width, None, axis=dim), axis, forward
        )
        high = lax.ppermute(lax.slice_in_dim(block, 0, width, axis=dim), axis, backward)
        block = jnp.concatenate([low, block, high], axis=dim)
    return block


def ring_pairs(count, steps):
    return [(source, (source + steps) % count) for source in range(count)]


def passed_along(value, axis, steps):
    count = lax.axis_size(axis)
    pairs = [(source, (source + steps) % count) for source in range(count)]
    return lax.ppermute(value, axis, pairs)


def extend(grouped):
    return with_halo(grouped, (("space", grouped.ndim - 1),), EDGE * GROUP_SITE_SPAN)


def pass_kernel(edge, idx_ref, cnt_ref, src_ref, op_ref, val_ref, wt_ref, *rest):
    if edge:
        acc_ref, out_ref = rest
    else:
        (out_ref,) = rest
    width = GROUP_SITE_SPAN
    fields = val_ref.shape[0]
    rows = src_ref.shape[0]
    blocks = op_ref.shape[0]
    low_blocks = EDGE
    own_blocks = out_ref.shape[1] // width - 2 * EDGE
    period = 8
    if edge:
        out_ref[...] = acc_ref[...]
    else:
        out_ref[...] = jnp.zeros_like(out_ref)
    count = cnt_ref[0]
    lane = lax.broadcasted_iota(jnp.int32, (1, width), 1)
    for k in range(blocks):
        index = idx_ref[k]
        inside = jnp.logical_and(index >= low_blocks, index < low_blocks + own_blocks)
        take = jnp.logical_not(inside) if edge else inside

        @pl.when(take)
        def _():
            if edge:
                column = jnp.where(index < low_blocks, index, index - own_blocks)
            else:
                column = index - low_blocks
            x = src_ref[:, pl.ds(pl.multiple_of(column * width, width), width)]
            op = op_ref[k]
            images = lax.dot_general(
                x, op, (((1,), (1,)), ((), ())), preferred_element_type=jnp.float32
            ).reshape(rows // period, period, width)
            observed = val_ref[:, k * width:(k + 1) * width].astype(jnp.float32)
            observed = jnp.concatenate([observed] * (period // fields), axis=0)[None]
            live = (k * width + lane) < count
            scaling = jnp.where(live, wt_ref[:, k * width:(k + 1) * width].astype(jnp.float32), 0.0)
            scaling = jnp.concatenate([scaling] * (period // fields), axis=0)[None]
            misfit = ((images - observed) * scaling).reshape(rows, width).astype(jnp.bfloat16)
            start = pl.multiple_of(index * width, width)
            out_ref[:, pl.ds(start, width)] += jnp.dot(
                misfit, op, preferred_element_type=jnp.float32
            )


def observe_pass(edge, src, operator, indices, values, weights, counts, acc, cells):
    rows = src.shape[0]
    full = lambda *a: pl.BlockSpec(memory_space=pltpu.VMEM)
    operands = [indices, counts, src, operator, values, weights] + ([acc] if edge else [])
    flops = 2 * operator.shape[0] * rows * GROUP_SITE_SPAN * GROUP_SITE_SPAN
    return pl.pallas_call(
        functools.partial(pass_kernel, edge),
        in_specs=[pl.BlockSpec(memory_space=pltpu.SMEM)] * 2 + [full()] * (len(operands) - 2),
        out_specs=full(),
        out_shape=jax.ShapeDtypeStruct((rows, cells), jnp.float32),
        cost_estimate=pl.CostEstimate(
            flops=flops, bytes_accessed=operator.size * 2 + rows * cells * 8, transcendentals=0
        ),
    )(*operands)


def settle(adjoint_ext):
    rim_width = EDGE * GROUP_SITE_SPAN
    lower_rim = adjoint_ext[..., :rim_width]
    upper_rim = adjoint_ext[..., -rim_width:]
    interior = adjoint_ext[..., rim_width:-rim_width]
    from_above = passed_along(lower_rim, "space", -1)
    from_below = passed_along(upper_rim, "space", 1)
    interior = interior.at[..., -rim_width:].add(from_above)
    return interior.at[..., :rim_width].add(from_below)


def body(hindcast_archive, op_blocks, block_index, obs_values, obs_weights, obs_counts):
    ring = lax.axis_size("tq")
    here = lax.axis_index("tq")
    own = hindcast_archive[0]
    leads, members, fields, cells = own.shape
    own = own.reshape(leads, members * fields, cells)
    outgoing = jnp.roll(own, here, axis=0)
    incoming = lax.all_to_all(outgoing, "tq", 0, 0, tiled=True)
    rim = EDGE * GROUP_SITE_SPAN
    space = lax.axis_size("space")
    rows = leads * members * fields
    width = cells + 2 * rim
    args = (op_blocks[0], block_index[0], obs_values[0], obs_weights[0], obs_counts[0])
    low = lax.ppermute(incoming[..., cells - rim:], "space", ring_pairs(space, 1))
    high = lax.ppermute(incoming[..., :rim], "space", ring_pairs(space, -1))
    partial = observe_pass(False, incoming.reshape(rows, cells), *args, None, width)
    rims = jnp.concatenate([low.reshape(rows, rim), high.reshape(rows, rim)], axis=1)
    adjoint_rows = observe_pass(True, rims, *args, partial, width)
    interior = settle(adjoint_rows.reshape(1, leads, members * fields, width))[0]
    returned = lax.all_to_all(interior, "tq", 0, 0, tiled=True)
    running = returned[0]
    for slot in range(1, ring):
        running = running + returned[slot]
    return running.reshape(1, members, fields, cells)


def solution(mesh):
    tm_size = mesh.shape["tm"]
    lead_count = 4
    devices = mesh.devices.reshape(lead_count, tm_size // lead_count, mesh.shape["space"])
    ring_mesh = Mesh(devices, ("tq", "tr", "space"))
    tm = ("tq", "tr")
    in_specs = (
        P(tm, None, None, None, "space"),
        P(tm, "space", None, None),
        P(tm, "space"),
        P(tm, None, "space"),
        P(tm, None, "space"),
        P(tm, "space"),
    )
    out_specs = P(tm, None, None, "space")
    return jax.shard_map(body, mesh=ring_mesh, in_specs=in_specs, out_specs=out_specs, check_vma=False)
```

```python
import functools

import jax
import jax.numpy as jnp
from jax import lax
from jax.experimental import pallas as pl
from jax.experimental.pallas import tpu as pltpu
from jax.sharding import Mesh
from jax.sharding import PartitionSpec as P

GROUP_SITE_SPAN = 128
EDGE = 2
BLOCKS_PER_STEP = 96


def with_halo(block, sides, width):
    for axis, dim in sides:
        count = lax.axis_size(axis)
        forward = [(i, i + 1) for i in range(count - 1)]
        forward.append((count - 1, 0))
        backward = [(target, source) for source, target in forward]
        low = lax.ppermute(
            lax.slice_in_dim(block, block.shape[dim] - width, None, axis=dim), axis, forward
        )
        high = lax.ppermute(lax.slice_in_dim(block, 0, width, axis=dim), axis, backward)
        block = jnp.concatenate([low, block, high], axis=dim)
    return block


def ring_pairs(count, steps):
    return [(source, (source + steps) % count) for source in range(count)]


def passed_along(value, axis, steps):
    count = lax.axis_size(axis)
    pairs = [(source, (source + steps) % count) for source in range(count)]
    return lax.ppermute(value, axis, pairs)


def extend(grouped):
    return with_halo(grouped, (("space", grouped.ndim - 1),), EDGE * GROUP_SITE_SPAN)


def observe_kernel(
    idx_ref, cnt_ref, low_ref, mid_ref, high_ref, op_ref, val_ref, wt_ref, out_ref, low_out, high_out, ext_ref,
):
    step = pl.program_id(0)
    width = GROUP_SITE_SPAN
    fields = val_ref.shape[0]
    rows = ext_ref.shape[0]
    rim = low_ref.shape[1]
    tile = mid_ref.shape[1]
    blocks = op_ref.shape[0]
    period = 8

    @pl.when(step == 0)
    def _():
        ext_ref[:, :rim] = low_ref[...]
        ext_ref[:, rim:rim + tile] = mid_ref[...]
        ext_ref[:, rim + tile:] = high_ref[...]
        out_ref[...] = jnp.zeros_like(out_ref)

    count = cnt_ref[0]
    lane = lax.broadcasted_iota(jnp.int32, (1, width), 1)

    def forward(k):
        b = step * blocks + k
        start = pl.multiple_of(idx_ref[b] * width, width)
        x = ext_ref[:, pl.ds(start, width)]
        op = op_ref[k]
        images = lax.dot_general(
            x, op, (((1,), (1,)), ((), ())), preferred_element_type=jnp.float32
        ).reshape(rows // period, period, width)
        observed = val_ref[:, k * width:(k + 1) * width].astype(jnp.float32)
        observed = jnp.concatenate([observed] * (period // fields), axis=0)[None]
        live = (b * width + lane) < count
        scaling = jnp.where(live, wt_ref[:, k * width:(k + 1) * width].astype(jnp.float32), 0.0)
        scaling = jnp.concatenate([scaling] * (period // fields), axis=0)[None]
        misfit = ((images - observed) * scaling).reshape(rows, width).astype(jnp.bfloat16)
        return start, misfit, op

    def backward(start, misfit, op):
        out_ref[:, pl.ds(start, width)] += jnp.dot(misfit, op, preferred_element_type=jnp.float32)

    pending = forward(0)
    for k in range(1, blocks):
        ahead = forward(k)
        backward(*pending)
        pending = ahead
    backward(*pending)
    low_out[...] = out_ref[:, :rim]
    high_out[...] = out_ref[:, rim + tile:]


def observe(low, mid, high, operator, indices, values, weights, counts):
    rows, tile = mid.shape
    rim = low.shape[1]
    cells = tile + 2 * rim
    obs_blocks = operator.shape[0]
    width = GROUP_SITE_SPAN
    fields = values.shape[0]
    steps = obs_blocks // BLOCKS_PER_STEP
    span = BLOCKS_PER_STEP * width
    whole = lambda g, i, c: (0, 0)
    grid_spec = pltpu.PrefetchScalarGridSpec(
        num_scalar_prefetch=2,
        grid=(steps,),
        in_specs=[
            pl.BlockSpec((rows, rim), whole),
            pl.BlockSpec((rows, tile), whole),
            pl.BlockSpec((rows, rim), whole),
            pl.BlockSpec((BLOCKS_PER_STEP, width, width), lambda g, i, c: (g, 0, 0)),
            pl.BlockSpec((fields, span), lambda g, i, c: (0, g)),
            pl.BlockSpec((fields, span), lambda g, i, c: (0, g)),
        ],
        out_specs=[
            pl.BlockSpec((rows, cells), whole),
            pl.BlockSpec((rows, rim), whole),
            pl.BlockSpec((rows, rim), whole),
        ],
        scratch_shapes=[pltpu.VMEM((rows, cells), mid.dtype)],
    )
    flops = 4 * obs_blocks * rows * width * width
    bytes_accessed = operator.size * 2 + rows * cells * 6 + values.size * 4
    return pl.pallas_call(
        observe_kernel,
        grid_spec=grid_spec,
        out_shape=[
            jax.ShapeDtypeStruct((rows, cells), jnp.float32),
            jax.ShapeDtypeStruct((rows, rim), jnp.float32),
            jax.ShapeDtypeStruct((rows, rim), jnp.float32),
        ],
        compiler_params=pltpu.CompilerParams(dimension_semantics=("arbitrary",)),
        cost_estimate=pl.CostEstimate(
            flops=flops, bytes_accessed=bytes_accessed, transcendentals=0
        ),
    )(indices, counts, low, mid, high, operator, values, weights)


def settle(adjoint_ext):
    rim_width = EDGE * GROUP_SITE_SPAN
    lower_rim = adjoint_ext[..., :rim_width]
    upper_rim = adjoint_ext[..., -rim_width:]
    interior = adjoint_ext[..., rim_width:-rim_width]
    from_above = passed_along(lower_rim, "space", -1)
    from_below = passed_along(upper_rim, "space", 1)
    interior = interior.at[..., -rim_width:].add(from_above)
    return interior.at[..., :rim_width].add(from_below)


def body(hindcast_archive, op_blocks, block_index, obs_values, obs_weights, obs_counts):
    ring = lax.axis_size("tq")
    here = lax.axis_index("tq")
    own = hindcast_archive[0]
    leads, members, fields, cells = own.shape
    own = own.reshape(leads, members * fields, cells)
    outgoing = jnp.roll(own, here, axis=0)
    incoming = lax.all_to_all(outgoing, "tq", 0, 0, tiled=True)
    rim = EDGE * GROUP_SITE_SPAN
    space = lax.axis_size("space")
    low = lax.ppermute(incoming[..., cells - rim:], "space", ring_pairs(space, 1))
    high = lax.ppermute(incoming[..., :rim], "space", ring_pairs(space, -1))
    width = cells + 2 * rim
    adjoint_rows, low_adj, high_adj = observe(
        low.reshape(leads * members * fields, rim),
        incoming.reshape(leads * members * fields, cells),
        high.reshape(leads * members * fields, rim),
        op_blocks[0],
        block_index[0],
        obs_values[0],
        obs_weights[0],
        obs_counts[0],
    )
    from_above = passed_along(low_adj.reshape(leads, members * fields, rim), "space", -1)
    from_below = passed_along(high_adj.reshape(leads, members * fields, rim), "space", 1)
    interior = adjoint_rows.reshape(leads, members * fields, width)[..., rim:rim + cells]
    interior = interior.at[..., cells - rim:].add(from_above)
    interior = interior.at[..., :rim].add(from_below)
    returned = lax.all_to_all(interior, "tq", 0, 0, tiled=True)
    running = returned[0]
    for slot in range(1, ring):
        running = running + returned[slot]
    return running.reshape(1, members, fields, cells)


def solution(mesh):
    tm_size = mesh.shape["tm"]
    lead_count = 4
    devices = mesh.devices.reshape(lead_count, tm_size // lead_count, mesh.shape["space"])
    ring_mesh = Mesh(devices, ("tq", "tr", "space"))
    tm = ("tq", "tr")
    in_specs = (
        P(tm, None, None, None, "space"),
        P(tm, "space", None, None),
        P(tm, "space"),
        P(tm, None, "space"),
        P(tm, None, "space"),
        P(tm, "space"),
    )
    out_specs = P(tm, None, None, "space")
    return jax.shard_map(body, mesh=ring_mesh, in_specs=in_specs, out_specs=out_specs, check_vma=False)
```

```python
import functools

import jax
import jax.numpy as jnp
from jax import lax
from jax.experimental import pallas as pl
from jax.experimental.pallas import tpu as pltpu
from jax.sharding import Mesh
from jax.sharding import PartitionSpec as P

GROUP_SITE_SPAN = 128
EDGE = 2
BLOCKS_PER_STEP = 96


def with_halo(block, sides, width):
    for axis, dim in sides:
        count = lax.axis_size(axis)
        forward = [(i, i + 1) for i in range(count - 1)]
        forward.append((count - 1, 0))
        backward = [(target, source) for source, target in forward]
        low = lax.ppermute(
            lax.slice_in_dim(block, block.shape[dim] - width, None, axis=dim), axis, forward
        )
        high = lax.ppermute(lax.slice_in_dim(block, 0, width, axis=dim), axis, backward)
        block = jnp.concatenate([low, block, high], axis=dim)
    return block


def ring_pairs(count, steps):
    return [(source, (source + steps) % count) for source in range(count)]


def passed_along(value, axis, steps):
    count = lax.axis_size(axis)
    pairs = [(source, (source + steps) % count) for source in range(count)]
    return lax.ppermute(value, axis, pairs)


def extend(grouped):
    return with_halo(grouped, (("space", grouped.ndim - 1),), EDGE * GROUP_SITE_SPAN)


def observe_kernel(
    idx_ref, cnt_ref, low_ref, mid_ref, high_ref, op_ref, val_ref, wt_ref, out_ref, low_out, high_out, ext_ref,
):
    step = pl.program_id(0)
    width = GROUP_SITE_SPAN
    fields = val_ref.shape[0]
    rows = ext_ref.shape[0]
    rim = low_ref.shape[1]
    tile = mid_ref.shape[1]
    blocks = op_ref.shape[0]
    period = 8

    @pl.when(step == 0)
    def _():
        ext_ref[:, :rim] = low_ref[...]
        ext_ref[:, rim:rim + tile] = mid_ref[...]
        ext_ref[:, rim + tile:] = high_ref[...]
        out_ref[...] = jnp.zeros_like(out_ref)

    count = cnt_ref[0]
    lane = lax.broadcasted_iota(jnp.int32, (1, width), 1)

    def forward(k):
        b = step * blocks + k
        start = pl.multiple_of(idx_ref[b] * width, width)
        x = ext_ref[:, pl.ds(start, width)]
        op = op_ref[k]
        images = lax.dot_general(
            x, op, (((1,), (1,)), ((), ())), preferred_element_type=jnp.float32
        ).reshape(rows // period, period, width)
        observed = val_ref[:, k * width:(k + 1) * width].astype(jnp.float32)
        observed = jnp.concatenate([observed] * (period // fields), axis=0)[None]
        live = (b * width + lane) < count
        scaling = jnp.where(live, wt_ref[:, k * width:(k + 1) * width].astype(jnp.float32), 0.0)
        scaling = jnp.concatenate([scaling] * (period // fields), axis=0)[None]
        misfit = ((images - observed) * scaling).reshape(rows, width).astype(jnp.bfloat16)
        return start, misfit, op

    def backward(start, misfit, op):
        out_ref[:, pl.ds(start, width)] += jnp.dot(misfit, op, preferred_element_type=jnp.float32)

    pending = [forward(0), forward(1)]
    for k in range(2, blocks):
        pending.append(forward(k))
        backward(*pending.pop(0))
    for item in pending:
        backward(*item)
    low_out[...] = out_ref[:, :rim]
    high_out[...] = out_ref[:, rim + tile:]


def observe(low, mid, high, operator, indices, values, weights, counts):
    rows, tile = mid.shape
    rim = low.shape[1]
    cells = tile + 2 * rim
    obs_blocks = operator.shape[0]
    width = GROUP_SITE_SPAN
    fields = values.shape[0]
    steps = obs_blocks // BLOCKS_PER_STEP
    span = BLOCKS_PER_STEP * width
    whole = lambda g, i, c: (0, 0)
    grid_spec = pltpu.PrefetchScalarGridSpec(
        num_scalar_prefetch=2,
        grid=(steps,),
        in_specs=[
            pl.BlockSpec((rows, rim), whole),
            pl.BlockSpec((rows, tile), whole),
            pl.BlockSpec((rows, rim), whole),
            pl.BlockSpec((BLOCKS_PER_STEP, width, width), lambda g, i, c: (g, 0, 0)),
            pl.BlockSpec((fields, span), lambda g, i, c: (0, g)),
            pl.BlockSpec((fields, span), lambda g, i, c: (0, g)),
        ],
        out_specs=[
            pl.BlockSpec((rows, cells), whole),
            pl.BlockSpec((rows, rim), whole),
            pl.BlockSpec((rows, rim), whole),
        ],
        scratch_shapes=[pltpu.VMEM((rows, cells), mid.dtype)],
    )
    flops = 4 * obs_blocks * rows * width * width
    bytes_accessed = operator.size * 2 + rows * cells * 6 + values.size * 4
    return pl.pallas_call(
        observe_kernel,
        grid_spec=grid_spec,
        out_shape=[
            jax.ShapeDtypeStruct((rows, cells), jnp.float32),
            jax.ShapeDtypeStruct((rows, rim), jnp.float32),
            jax.ShapeDtypeStruct((rows, rim), jnp.float32),
        ],
        compiler_params=pltpu.CompilerParams(dimension_semantics=("arbitrary",)),
        cost_estimate=pl.CostEstimate(
            flops=flops, bytes_accessed=bytes_accessed, transcendentals=0
        ),
    )(indices, counts, low, mid, high, operator, values, weights)


def settle(adjoint_ext):
    rim_width = EDGE * GROUP_SITE_SPAN
    lower_rim = adjoint_ext[..., :rim_width]
    upper_rim = adjoint_ext[..., -rim_width:]
    interior = adjoint_ext[..., rim_width:-rim_width]
    from_above = passed_along(lower_rim, "space", -1)
    from_below = passed_along(upper_rim, "space", 1)
    interior = interior.at[..., -rim_width:].add(from_above)
    return interior.at[..., :rim_width].add(from_below)


def body(hindcast_archive, op_blocks, block_index, obs_values, obs_weights, obs_counts):
    ring = lax.axis_size("tq")
    here = lax.axis_index("tq")
    own = hindcast_archive[0]
    leads, members, fields, cells = own.shape
    own = own.reshape(leads, members * fields, cells)
    outgoing = jnp.roll(own, here, axis=0)
    incoming = lax.all_to_all(outgoing, "tq", 0, 0, tiled=True)
    rim = EDGE * GROUP_SITE_SPAN
    space = lax.axis_size("space")
    low = lax.ppermute(incoming[..., cells - rim:], "space", ring_pairs(space, 1))
    high = lax.ppermute(incoming[..., :rim], "space", ring_pairs(space, -1))
    width = cells + 2 * rim
    adjoint_rows, low_adj, high_adj = observe(
        low.reshape(leads * members * fields, rim),
        incoming.reshape(leads * members * fields, cells),
        high.reshape(leads * members * fields, rim),
        op_blocks[0],
        block_index[0],
        obs_values[0],
        obs_weights[0],
        obs_counts[0],
    )
    from_above = passed_along(low_adj.reshape(leads, members * fields, rim), "space", -1)
    from_below = passed_along(high_adj.reshape(leads, members * fields, rim), "space", 1)
    interior = adjoint_rows.reshape(leads, members * fields, width)[..., rim:rim + cells]
    interior = interior.at[..., cells - rim:].add(from_above)
    interior = interior.at[..., :rim].add(from_below)
    returned = lax.all_to_all(interior, "tq", 0, 0, tiled=True)
    running = returned[0]
    for slot in range(1, ring):
        running = running + returned[slot]
    return running.reshape(1, members, fields, cells)


def solution(mesh):
    tm_size = mesh.shape["tm"]
    lead_count = 4
    devices = mesh.devices.reshape(lead_count, tm_size // lead_count, mesh.shape["space"])
    ring_mesh = Mesh(devices, ("tq", "tr", "space"))
    tm = ("tq", "tr")
    in_specs = (
        P(tm, None, None, None, "space"),
        P(tm, "space", None, None),
        P(tm, "space"),
        P(tm, None, "space"),
        P(tm, None, "space"),
        P(tm, "space"),
    )
    out_specs = P(tm, None, None, "space")
    return jax.shard_map(body, mesh=ring_mesh, in_specs=in_specs, out_specs=out_specs, check_vma=False)
```
